512 devices in a mesh: ens: 4 (over z_hi), lon: 32 (over z_lo, y, core), lat: 4 (over x).
Axes of the slice: x: 4, y: 8, z: 8 (z_hi: 4, z_lo: 2; z = z_hi * 2 + z_lo), core: 2. Of those that a mesh axis runs over, the one named last changes fastest.
Arguments:
- ocean_state: bfloat16 [4, 200, 32, 4096], P('ens', None, 'lat', 'lon'), may hold values from -6 to 6
- ocean_mask: int32 [32, 4096], P('lat', 'lon'), may hold values from 0 to 1, as said below
- dw_weight: float32 [200, 49], replicated, may hold values from -0.875 to 0.875
- norm_gain: float32 [200], replicated, may hold values from 0.1 to 1.9
- expand_weight: bfloat16 [200, 800], replicated, may hold values from -0.4375 to 0.4375
- reduce_weight: bfloat16 [800, 200], replicated, may hold values from -0.21875 to 0.21875
- cotangent: bfloat16 [4, 200, 32, 4096], P('ens', None, 'lat', 'lon'), may hold values from -6 to 6
Outputs:
- next_state: bfloat16 [4, 200, 32, 4096], P('ens', None, 'lat', 'lon')
- grad_depthwise: float32 [200, 49], replicated
- grad_gain: float32 [200], replicated
- grad_expand: float32 [200, 800], replicated
- grad_reduce: float32 [800, 200], replicated
The draws below stay inside these ranges and needn't reach their ends.
Inputs may be any that keep to these rules, and one draw needn't show every extreme that they name: `ocean_mask`: the share of ocean cells differs from tile to tile of 8 x 128 cells, from about a third to nearly all.
All inputs are finite; a program needn't handle non-finite values.
Results may differ from the reference program's by a relative error of at most 0.0058.
Values may be sent and summed in bfloat16 or wider, within the bound.
No kernel may reach another device: no remote copies, remote signals or barrier semaphores. Data moves between devices by JAX's collectives and lax.ppermute only.
A program may use at most 64 MiB of HBM per device.

```python
import math
import jax
import jax.numpy as jnp
from jax import lax

C = 200
HID = 800
KS = 7
TH = 8
TW = 128
ENS = 4
NY = 32
NX = 4096


def draw_ocean_mask(key, part):
    tile_key = jax.random.fold_in(key, 11)
    cell_key = jax.random.fold_in(key, 12)
    ocean_share = jax.random.randint(tile_key, (NY // TH, NX // TW), 30, 101)
    ocean_share = jnp.repeat(jnp.repeat(ocean_share, TH, axis=0), TW, axis=1)
    cell_draw = jax.random.randint(cell_key, (NY, NX), 0, 100)
    return jnp.where(cell_draw < ocean_share, 1, 0).astype(jnp.int32)


def shard_levels(rng, shape, cuts, smallest, high):
    def one(axis_at, blocks):
        heights = jax.random.uniform(jax.random.fold_in(jax.random.fold_in(rng, 6), axis_at), (blocks,), jnp.float32, smallest / len(cuts), high / len(cuts))
        return jnp.repeat(jnp.exp(heights), shape[axis_at] // blocks).reshape((-1,) + (1,) * (len(shape) - axis_at - 1))

    level = one(*cuts[0])
    for cut in cuts[1:]:
        level = level * one(*cut)
    return level


def gaussian(own_key, extent, scale, most, split=(), dtype=jnp.bfloat16):
    array = jax.random.normal(own_key, extent, jnp.float32) * scale
    if len(split) > 0:
        array = shard_levels(own_key, extent, split, -0.22, 0.18) * array
    return jnp.clip(array, min=-most, max=most).astype(dtype)


def setup_inputs(seed: int = 0) -> dict:
    streams_of = jax.random.split(jax.random.key(seed), 8)
    return {
        "ocean_state": gaussian(streams_of[0], (ENS, C, NY, NX), 1.0, 6.0, ((0, 4), (2, 4), (3, 32))),
        "ocean_mask": draw_ocean_mask(jax.random.fold_in(streams_of[7], 71), 0),
        "dw_weight": gaussian(streams_of[2], (C, KS * KS), (KS * KS) ** -0.5, 0.875, (), jnp.float32),
        "norm_gain": jnp.clip(1.0 + 0.18 * jax.random.normal(streams_of[3], (C,), jnp.float32), 0.1, 1.9),
        "expand_weight": gaussian(streams_of[4], (C, HID), C ** -0.5, 0.4375),
        "reduce_weight": gaussian(streams_of[5], (HID, C), HID ** -0.5, 0.21875),
        "cotangent": gaussian(streams_of[6], (ENS, C, NY, NX), 1.0, 6.0, ((0, 4), (2, 4), (3, 32))),
    }


norm_eps = 1e-06
root_half = 0.7071067811865476
gauss_norm = 0.3989422804014327

def pad_global(field_in):
    margin = KS // 2
    wrapped = jnp.concatenate([field_in[:, :, NX - margin:], field_in, field_in[:, :, :margin]], axis=2)
    north_rows = wrapped[:, NY - margin:, :][:, ::-1, ::-1]
    south_rows = jnp.zeros_like(north_rows)
    return jnp.concatenate([south_rows, wrapped, north_rows], axis=1)

def depthwise(padded, dw_weight, out_rows, out_cols):
    conv_sum = jnp.zeros((padded.shape[0], out_rows, out_cols), jnp.float32)
    for shift_a in range(KS):
        for shift_b in range(KS):
            tap_weight = dw_weight[:, shift_a * KS + shift_b][:, None, None]
            window = padded[:, shift_a:shift_a + out_rows, shift_b:shift_b + out_cols].astype(jnp.float32)
            conv_sum = conv_sum + tap_weight * window
    return conv_sum

def depthwise_grad(d_conv, padded, out_rows, out_cols):
    columns = []
    for shift_a in range(KS):
        for shift_b in range(KS):
            window = padded[:, shift_a:shift_a + out_rows, shift_b:shift_b + out_cols].astype(jnp.float32)
            columns.append(lax.optimization_barrier(jnp.sum(d_conv * window, axis=(1, 2))))
    return jnp.stack(columns, axis=1)

def cell_pass(conv_blk, state_blk, cot_blk, mask_blk, norm_gain, expand_weight, reduce_weight):
    chan_mean = lax.optimization_barrier(jnp.mean(conv_blk, axis=0, keepdims=True))
    centred = conv_blk - chan_mean
    chan_var = lax.optimization_barrier(jnp.mean(centred * centred, axis=0, keepdims=True))
    inv_std = lax.rsqrt(chan_var + norm_eps)
    normed = centred * inv_std
    scaled = (normed * norm_gain[:, None]).astype(jnp.bfloat16)
    pre_act = jnp.dot(expand_weight.T, scaled, preferred_element_type=jnp.float32)
    normal_cdf = 0.5 * (1.0 + lax.erf(pre_act * root_half))
    normal_pdf = jnp.exp(-0.5 * pre_act * pre_act) * gauss_norm
    hidden = (pre_act * normal_cdf).astype(jnp.bfloat16)
    gelu_slope = normal_cdf + pre_act * normal_pdf
    branch = jnp.dot(reduce_weight.T, hidden, preferred_element_type=jnp.float32)
    out_blk = ((state_blk.astype(jnp.float32) + branch) * mask_blk[None, :]).astype(jnp.bfloat16)
    grad_reduce = jnp.dot(hidden, cot_blk.T, preferred_element_type=jnp.float32)
    d_hidden = jnp.dot(reduce_weight, cot_blk, preferred_element_type=jnp.float32)
    d_pre = (d_hidden * gelu_slope).astype(jnp.bfloat16)
    grad_expand = jnp.dot(scaled, d_pre.T, preferred_element_type=jnp.float32)
    d_scaled = jnp.dot(expand_weight, d_pre, preferred_element_type=jnp.float32)
    grad_gain = lax.optimization_barrier(jnp.sum(d_scaled * normed, axis=1))
    d_normed = d_scaled * norm_gain[:, None]
    d_conv = inv_std * (d_normed - lax.optimization_barrier(jnp.mean(d_normed, axis=0, keepdims=True)) - normed * lax.optimization_barrier(jnp.mean(d_normed * normed, axis=0, keepdims=True)))
    return (out_blk, d_conv, grad_expand, grad_reduce, grad_gain)

def member_pass(state_one, cot_one, ocean_mask, dw_weight, norm_gain, expand_weight, reduce_weight):
    mask_bf = ocean_mask.astype(jnp.bfloat16)
    masked = state_one * mask_bf[None]
    padded = pad_global(masked)
    conv_out = depthwise(padded, dw_weight, NY, NX)
    cells_all = NY * NX
    block_count = NY // TH * (NX // TW)
    block_len = cells_all // block_count

    def to_blocks(array_in):
        return array_in.reshape(array_in.shape[0], block_count, block_len).transpose(1, 0, 2)
    conv_blocks = to_blocks(conv_out.reshape(C, cells_all))
    state_blocks = to_blocks(state_one.reshape(C, cells_all))
    cot_blocks = to_blocks((cot_one * mask_bf[None]).reshape(C, cells_all))
    mask_blocks = ocean_mask.astype(jnp.float32).reshape(block_count, block_len)

    def block_step(carry, pieces):
        out_blk, d_conv, grad_expand, grad_reduce, grad_gain = cell_pass(pieces[0], pieces[1], pieces[2], pieces[3], norm_gain, expand_weight, reduce_weight)
        return ((carry[0] + grad_expand, carry[1] + grad_reduce, carry[2] + grad_gain), (out_blk, d_conv))
    start = (jnp.zeros((C, HID), jnp.float32), jnp.zeros((HID, C), jnp.float32), jnp.zeros((C,), jnp.float32))
    totals, stacked = lax.scan(block_step, start, (conv_blocks, state_blocks, cot_blocks, mask_blocks))
    out_full = stacked[0].transpose(1, 0, 2).reshape(C, NY, NX)
    d_conv_full = stacked[1].transpose(1, 0, 2).reshape(C, NY, NX)
    grad_depthwise = depthwise_grad(d_conv_full, padded, NY, NX)
    return (out_full, totals[0], totals[1], totals[2], grad_depthwise)

def reference(ocean_state, ocean_mask, dw_weight, norm_gain, expand_weight, reduce_weight, cotangent):

    def one_member(pair):
        return member_pass(pair[0], pair[1], ocean_mask, dw_weight, norm_gain, expand_weight, reduce_weight)
    results = lax.map(one_member, (ocean_state, cotangent))
    grad_scale = 1.0 / math.sqrt(ENS * NY * NX)
    next_state = results[0]
    grad_expand = lax.optimization_barrier(jnp.sum(results[1], axis=0)) * grad_scale
    grad_reduce = lax.optimization_barrier(jnp.sum(results[2], axis=0)) * grad_scale
    grad_gain = lax.optimization_barrier(jnp.sum(results[3], axis=0)) * grad_scale
    grad_depthwise = lax.optimization_barrier(jnp.sum(results[4], axis=0)) * grad_scale
    return (next_state, grad_depthwise, grad_gain, grad_expand, grad_reduce)
```

```python
import math

import jax
import jax.numpy as jnp
from jax import lax
from jax.sharding import PartitionSpec as P

KS = 7


norm_eps = 1e-06
root_half = 0.7071067811865476
gauss_norm = 0.3989422804014327


def with_halo(cells, sides, width):
    for axis, dim in sides:
        count = lax.axis_size(axis)
        head = lax.slice_in_dim(cells, 0, width, axis=dim)
        tail = lax.slice_in_dim(cells, cells.shape[dim] - width, cells.shape[dim], axis=dim)
        cells = jnp.concatenate(
            [
                lax.ppermute(tail, axis, [(i, (i + 1) % count) for i in range(count)]),
                cells,
                lax.ppermute(head, axis, [((i + 1) % count, i) for i in range(count)]),
            ],
            axis=dim,
        )
    return cells


def swapped(array, axis, stride):
    return lax.ppermute(array, axis, [(i, i ^ 1 << stride) for i in range(lax.axis_size(axis))])


def mirrored_across(array, axis):
    count = lax.axis_size(axis)
    return lax.ppermute(array, axis, [(i, count - 1 - i) for i in range(count)])


REDUCE_ORDER = (
    ("lon", 0), ("lat", 0), ("lon", 1), ("ens", 0), ("lon", 4),
    ("lat", 1), ("lon", 2), ("ens", 1), ("lon", 3),
)


def tree_psum(flat, steps, gather_dtype):
    halved = []
    for axis, bit in steps:
        if (1 << bit) >= lax.axis_size(axis):
            continue
        upper = (lax.axis_index(axis) >> bit) & 1
        if flat.shape[0] % 16 == 0:
            half = flat.shape[0] // 2
            low, high = flat[:half], flat[half:]
            keep = jnp.where(upper == 0, low, high)
            send = jnp.where(upper == 0, high, low)
            flat = keep + swapped(send, axis, bit)
            halved.append((axis, bit))
        else:
            flat = flat + swapped(flat, axis, bit)
    flat = flat.astype(gather_dtype)
    for axis, bit in reversed(halved):
        upper = (lax.axis_index(axis) >> bit) & 1
        other = swapped(flat, axis, bit)
        flat = jnp.where(
            upper == 0, jnp.concatenate([flat, other]), jnp.concatenate([other, flat])
        )
    return flat.astype(jnp.float32)


def depthwise(padded, dw_weight, out_rows, out_cols):
    conv_sum = jnp.zeros((padded.shape[0], out_rows, out_cols), jnp.float32)
    for shift_a in range(KS):
        for shift_b in range(KS):
            tap_weight = dw_weight[:, shift_a * KS + shift_b][:, None, None]
            window = padded[:, shift_a : shift_a + out_rows, shift_b : shift_b + out_cols].astype(
                jnp.float32
            )
            conv_sum = conv_sum + tap_weight * window
    return conv_sum


def depthwise_grad(d_conv, padded, out_rows, out_cols):
    columns = []
    for shift_a in range(KS):
        for shift_b in range(KS):
            window = padded[:, shift_a : shift_a + out_rows, shift_b : shift_b + out_cols].astype(
                jnp.float32
            )
            columns.append(jnp.sum(d_conv * window, axis=(1, 2)))
    return jnp.stack(columns, axis=1)


def cell_pass(conv_blk, state_blk, cot_blk, mask_blk, norm_gain, expand_weight, reduce_weight):
    chan_mean = jnp.mean(conv_blk, axis=0, keepdims=True)
    centred = conv_blk - chan_mean
    chan_var = jnp.mean(centred * centred, axis=0, keepdims=True)
    inv_std = lax.rsqrt(chan_var + norm_eps)
    normed = centred * inv_std
    scaled = (normed * norm_gain[:, None]).astype(jnp.bfloat16)
    pre_act = jnp.dot(expand_weight.T, scaled, preferred_element_type=jnp.float32)
    normal_cdf = 0.5 * (1.0 + lax.erf(pre_act * root_half))
    normal_pdf = jnp.exp(-0.5 * pre_act * pre_act) * gauss_norm
    hidden = (pre_act * normal_cdf).astype(jnp.bfloat16)
    gelu_slope = normal_cdf + pre_act * normal_pdf
    branch = jnp.dot(reduce_weight.T, hidden, preferred_element_type=jnp.float32)
    out_blk = ((state_blk.astype(jnp.float32) + branch) * mask_blk[None, :]).astype(jnp.bfloat16)
    grad_reduce = jnp.dot(hidden, cot_blk.T, preferred_element_type=jnp.float32)
    d_hidden = jnp.dot(reduce_weight, cot_blk, preferred_element_type=jnp.float32)
    d_pre = (d_hidden * gelu_slope).astype(jnp.bfloat16)
    grad_expand = jnp.dot(scaled, d_pre.T, preferred_element_type=jnp.float32)
    d_scaled = jnp.dot(expand_weight, d_pre, preferred_element_type=jnp.float32)
    grad_gain = jnp.sum(d_scaled * normed, axis=1)
    d_normed = d_scaled * norm_gain[:, None]
    d_conv = inv_std * (
        d_normed
        - jnp.mean(d_normed, axis=0, keepdims=True)
        - normed * jnp.mean(d_normed * normed, axis=0, keepdims=True)
    )
    return (out_blk, d_conv, grad_expand, grad_reduce, grad_gain)


def body(ocean_state, ocean_mask, dw_weight, norm_gain, expand_weight, reduce_weight, cotangent):
    state_tile = ocean_state[0]
    channels = state_tile.shape[0]
    tile_rows = state_tile.shape[1]
    tile_cols = state_tile.shape[2]
    margin = KS // 2
    mask_bf = ocean_mask.astype(jnp.bfloat16)
    masked = state_tile * mask_bf[None]
    padded = with_halo(masked, (("lon", 2), ("lat", 1)), margin)
    lat_now = lax.axis_index("lat")
    lat_count = lax.axis_size("lat")
    lon_count = lax.axis_size("lon")
    top_strip = padded[:, tile_rows : tile_rows + margin, :][:, ::-1, ::-1]
    mirrored = mirrored_across(top_strip, "lon")
    north_rows = jnp.where(lat_now == lat_count - 1, mirrored, padded[:, tile_rows + margin :, :])
    south_rows = jnp.where(lat_now == 0, jnp.zeros_like(top_strip), padded[:, :margin, :])
    padded = jnp.concatenate(
        [south_rows, padded[:, margin : tile_rows + margin, :], north_rows], axis=1
    )
    conv_out = depthwise(padded, dw_weight, tile_rows, tile_cols)
    cell_count = tile_rows * tile_cols
    cot_masked = (cotangent[0] * mask_bf[None]).reshape(channels, cell_count)
    out_flat, d_conv, grad_expand, grad_reduce, grad_gain = cell_pass(
        conv_out.reshape(channels, cell_count),
        state_tile.reshape(channels, cell_count),
        cot_masked,
        ocean_mask.astype(jnp.float32).reshape(cell_count),
        norm_gain,
        expand_weight,
        reduce_weight,
    )
    grad_depthwise = depthwise_grad(
        d_conv.reshape(channels, tile_rows, tile_cols), padded, tile_rows, tile_cols
    )
    grad_scale = 1.0 / math.sqrt(lax.axis_size("ens") * lat_count * lon_count * cell_count)
    grad_expand = grad_expand * grad_scale
    grad_reduce = grad_reduce * grad_scale
    grad_gain = grad_gain * grad_scale
    grad_depthwise = grad_depthwise * grad_scale
    pieces = (grad_expand, grad_reduce, grad_gain, grad_depthwise)
    flat = jnp.concatenate([piece.reshape(-1) for piece in pieces])
    lanes = 128
    rows = -(-flat.shape[0] // (lanes * 256)) * 256
    flat = jnp.pad(flat, (0, rows * lanes - flat.shape[0])).reshape(rows, lanes)
    steps = [(axis, bit) for axis, bit in REDUCE_ORDER]
    for axis in ("ens", "lon", "lat"):
        for bit in range(lax.axis_size(axis).bit_length() - 1):
            if (axis, bit) not in steps:
                steps.append((axis, bit))
    flat = tree_psum(flat, steps, jnp.float32).reshape(-1)
    summed = []
    offset = 0
    for piece in pieces:
        summed.append(flat[offset : offset + piece.size].reshape(piece.shape))
        offset += piece.size
    grad_expand, grad_reduce, grad_gain, grad_depthwise = summed
    next_state = out_flat.reshape(channels, tile_rows, tile_cols)[None]
    return (next_state, grad_depthwise, grad_gain, grad_expand, grad_reduce)


def solution(mesh):
    return jax.shard_map(
        body,
        mesh=mesh,
        in_specs=(
            P("ens", None, "lat", "lon"),
            P("lat", "lon"),
            P(),
            P(),
            P(),
            P(),
            P("ens", None, "lat", "lon"),
        ),
        out_specs=(P("ens", None, "lat", "lon"), P(), P(), P(), P()),
        check_vma=False,
    )
```

```python
import math

import jax
import jax.numpy as jnp
from jax import lax
from jax.sharding import PartitionSpec as P

KS = 7


norm_eps = 1e-06
root_half = 0.7071067811865476
gauss_norm = 0.3989422804014327


def with_halo(cells, sides, width):
    for axis, dim in sides:
        count = lax.axis_size(axis)
        head = lax.slice_in_dim(cells, 0, width, axis=dim)
        tail = lax.slice_in_dim(cells, cells.shape[dim] - width, cells.shape[dim], axis=dim)
        cells = jnp.concatenate(
            [
                lax.ppermute(tail, axis, [(i, (i + 1) % count) for i in range(count)]),
                cells,
                lax.ppermute(head, axis, [((i + 1) % count, i) for i in range(count)]),
            ],
            axis=dim,
        )
    return cells


def swapped(array, axis, stride):
    return lax.ppermute(array, axis, [(i, i ^ 1 << stride) for i in range(lax.axis_size(axis))])


def mirrored_across(array, axis):
    count = lax.axis_size(axis)
    return lax.ppermute(array, axis, [(i, count - 1 - i) for i in range(count)])


REDUCE_ORDER = (
    ("lon", 0), ("lat", 0), ("lon", 1), ("lon", 4), ("lat", 1),
    ("lon", 2), ("ens", 0), ("lon", 3), ("ens", 1),
)


def tree_psum(flat, steps, gather_dtype):
    halved = []
    for axis, bit in steps:
        if (1 << bit) >= lax.axis_size(axis):
            continue
        upper = (lax.axis_index(axis) >> bit) & 1
        if flat.shape[0] % 2 == 0 and flat.shape[0] >= 8:
            half = flat.shape[0] // 2
            low, high = flat[:half], flat[half:]
            keep = jnp.where(upper == 0, low, high)
            send = jnp.where(upper == 0, high, low)
            flat = keep + swapped(send, axis, bit)
            halved.append((axis, bit))
        else:
            flat = flat + swapped(flat, axis, bit)
    flat = flat.astype(gather_dtype)
    for axis, bit in reversed(halved):
        upper = (lax.axis_index(axis) >> bit) & 1
        other = swapped(flat, axis, bit)
        flat = jnp.where(
            upper == 0, jnp.concatenate([flat, other]), jnp.concatenate([other, flat])
        )
    return flat.astype(jnp.float32)


def depthwise(padded, dw_weight, out_rows, out_cols):
    conv_sum = jnp.zeros((padded.shape[0], out_rows, out_cols), jnp.float32)
    for shift_a in range(KS):
        for shift_b in range(KS):
            tap_weight = dw_weight[:, shift_a * KS + shift_b][:, None, None]
            window = padded[:, shift_a : shift_a + out_rows, shift_b : shift_b + out_cols].astype(
                jnp.float32
            )
            conv_sum = conv_sum + tap_weight * window
    return conv_sum


def depthwise_grad(d_conv, padded, out_rows, out_cols):
    columns = []
    for shift_a in range(KS):
        for shift_b in range(KS):
            window = padded[:, shift_a : shift_a + out_rows, shift_b : shift_b + out_cols].astype(
                jnp.float32
            )
            columns.append(jnp.sum(d_conv * window, axis=(1, 2)))
    return jnp.stack(columns, axis=1)


def cell_pass(conv_blk, state_blk, cot_blk, mask_blk, norm_gain, expand_weight, reduce_weight):
    chan_mean = jnp.mean(conv_blk, axis=0, keepdims=True)
    centred = conv_blk - chan_mean
    chan_var = jnp.mean(centred * centred, axis=0, keepdims=True)
    inv_std = lax.rsqrt(chan_var + norm_eps)
    normed = centred * inv_std
    scaled = (normed * norm_gain[:, None]).astype(jnp.bfloat16)
    pre_act = jnp.dot(expand_weight.T, scaled, preferred_element_type=jnp.float32)
    normal_cdf = 0.5 * (1.0 + lax.erf(pre_act * root_half))
    normal_pdf = jnp.exp(-0.5 * pre_act * pre_act) * gauss_norm
    hidden = (pre_act * normal_cdf).astype(jnp.bfloat16)
    gelu_slope = normal_cdf + pre_act * normal_pdf
    branch = jnp.dot(reduce_weight.T, hidden, preferred_element_type=jnp.float32)
    out_blk = ((state_blk.astype(jnp.float32) + branch) * mask_blk[None, :]).astype(jnp.bfloat16)
    grad_reduce = jnp.dot(hidden, cot_blk.T, preferred_element_type=jnp.float32)
    d_hidden = jnp.dot(reduce_weight, cot_blk, preferred_element_type=jnp.float32)
    d_pre = (d_hidden * gelu_slope).astype(jnp.bfloat16)
    grad_expand = jnp.dot(scaled, d_pre.T, preferred_element_type=jnp.float32)
    d_scaled = jnp.dot(expand_weight, d_pre, preferred_element_type=jnp.float32)
    grad_gain = jnp.sum(d_scaled * normed, axis=1)
    d_normed = d_scaled * norm_gain[:, None]
    d_conv = inv_std * (
        d_normed
        - jnp.mean(d_normed, axis=0, keepdims=True)
        - normed * jnp.mean(d_normed * normed, axis=0, keepdims=True)
    )
    return (out_blk, d_conv, grad_expand, grad_reduce, grad_gain)


def body(ocean_state, ocean_mask, dw_weight, norm_gain, expand_weight, reduce_weight, cotangent):
    state_tile = ocean_state[0]
    channels = state_tile.shape[0]
    tile_rows = state_tile.shape[1]
    tile_cols = state_tile.shape[2]
    margin = KS // 2
    mask_bf = ocean_mask.astype(jnp.bfloat16)
    masked = state_tile * mask_bf[None]
    padded = with_halo(masked, (("lon", 2), ("lat", 1)), margin)
    lat_now = lax.axis_index("lat")
    lat_count = lax.axis_size("lat")
    lon_count = lax.axis_size("lon")
    top_strip = padded[:, tile_rows : tile_rows + margin, :][:, ::-1, ::-1]
    mirrored = mirrored_across(top_strip, "lon")
    north_rows = jnp.where(lat_now == lat_count - 1, mirrored, padded[:, tile_rows + margin :, :])
    south_rows = jnp.where(lat_now == 0, jnp.zeros_like(top_strip), padded[:, :margin, :])
    padded = jnp.concatenate(
        [south_rows, padded[:, margin : tile_rows + margin, :], north_rows], axis=1
    )
    conv_out = depthwise(padded, dw_weight, tile_rows, tile_cols)
    cell_count = tile_rows * tile_cols
    cot_masked = (cotangent[0] * mask_bf[None]).reshape(channels, cell_count)
    out_flat, d_conv, grad_expand, grad_reduce, grad_gain = cell_pass(
        conv_out.reshape(channels, cell_count),
        state_tile.reshape(channels, cell_count),
        cot_masked,
        ocean_mask.astype(jnp.float32).reshape(cell_count),
        norm_gain,
        expand_weight,
        reduce_weight,
    )
    grad_depthwise = depthwise_grad(
        d_conv.reshape(channels, tile_rows, tile_cols), padded, tile_rows, tile_cols
    )
    grad_scale = 1.0 / math.sqrt(lax.axis_size("ens") * lat_count * lon_count * cell_count)
    grad_expand = grad_expand * grad_scale
    grad_reduce = grad_reduce * grad_scale
    grad_gain = grad_gain * grad_scale
    grad_depthwise = grad_depthwise * grad_scale
    width = grad_expand.shape[1]
    small = jnp.concatenate([grad_depthwise, grad_gain[:, None]], axis=1).reshape(-1)
    small_rows = -(-small.shape[0] // width)
    small_rows += -small_rows % 8
    small = jnp.pad(small, (0, small_rows * width - small.shape[0])).reshape(small_rows, width)
    packed = jnp.concatenate([grad_expand, grad_reduce.T, small], axis=0)
    steps = [(axis, bit) for axis, bit in REDUCE_ORDER]
    for axis in ("ens", "lon", "lat"):
        for bit in range(lax.axis_size(axis).bit_length() - 1):
            if (axis, bit) not in steps:
                steps.append((axis, bit))
    packed = tree_psum(packed, steps, jnp.float32)
    grad_expand = packed[:channels]
    grad_reduce = packed[channels : 2 * channels].T
    small = packed[2 * channels :].reshape(-1)[: channels * (KS * KS + 1)].reshape(channels, -1)
    grad_depthwise = small[:, : KS * KS]
    grad_gain = small[:, KS * KS]
    next_state = out_flat.reshape(channels, tile_rows, tile_cols)[None]
    return (next_state, grad_depthwise, grad_gain, grad_expand, grad_reduce)


def solution(mesh):
    return jax.shard_map(
        body,
        mesh=mesh,
        in_specs=(
            P("ens", None, "lat", "lon"),
            P("lat", "lon"),
            P(),
            P(),
            P(),
            P(),
            P("ens", None, "lat", "lon"),
        ),
        out_specs=(P("ens", None, "lat", "lon"), P(), P(), P(), P()),
        check_vma=False,
    )
```

```python
import math

import jax
import jax.numpy as jnp
from jax import lax
from jax.sharding import PartitionSpec as P

KS = 7


norm_eps = 1e-06
root_half = 0.7071067811865476
gauss_norm = 0.3989422804014327


def with_halo(cells, sides, width):
    for axis, dim in sides:
        count = lax.axis_size(axis)
        head = lax.slice_in_dim(cells, 0, width, axis=dim)
        tail = lax.slice_in_dim(cells, cells.shape[dim] - width, cells.shape[dim], axis=dim)
        cells = jnp.concatenate(
            [
                lax.ppermute(tail, axis, [(i, (i + 1) % count) for i in range(count)]),
                cells,
                lax.ppermute(head, axis, [((i + 1) % count, i) for i in range(count)]),
            ],
            axis=dim,
        )
    return cells


def swapped(array, axis, stride):
    return lax.ppermute(array, axis, [(i, i ^ 1 << stride) for i in range(lax.axis_size(axis))])


def mirrored_across(array, axis):
    count = lax.axis_size(axis)
    return lax.ppermute(array, axis, [(i, count - 1 - i) for i in range(count)])


REDUCE_ORDER = (
    ("lon", 0), ("lat", None), ("ens", None), ("lon", 1), ("lon", 4), ("lon", 2), ("lon", 3),
)


def spread(array, axis):
    count = lax.axis_size(axis)
    copies = jnp.broadcast_to(array[None], (count,) + array.shape)
    return lax.all_to_all(copies, axis, 0, 0, tiled=False)


def tree_psum(flat, steps, gather_dtype):
    scattered = []
    for axis, bit in steps:
        rows = flat.shape[0]
        if bit is None:
            count = lax.axis_size(axis)
            if rows % count == 0:
                chunks = flat.reshape((count, rows // count) + flat.shape[1:])
                flat = lax.all_to_all(chunks, axis, 0, 0, tiled=False).sum(0)
                scattered.append((axis, bit))
            else:
                flat = spread(flat, axis).sum(0)
            continue
        if (1 << bit) >= lax.axis_size(axis):
            continue
        upper = (lax.axis_index(axis) >> bit) & 1
        if rows % 2 == 0 and rows >= 8:
            half = rows // 2
            low, high = flat[:half], flat[half:]
            keep = jnp.where(upper == 0, low, high)
            send = jnp.where(upper == 0, high, low)
            flat = keep + swapped(send, axis, bit)
            scattered.append((axis, bit))
        else:
            flat = flat + swapped(flat, axis, bit)
    flat = flat.astype(gather_dtype)
    for axis, bit in reversed(scattered):
        if bit is None:
            gathered = spread(flat, axis)
            flat = gathered.reshape((-1,) + flat.shape[1:])
            continue
        upper = (lax.axis_index(axis) >> bit) & 1
        other = swapped(flat, axis, bit)
        flat = jnp.where(
            upper == 0, jnp.concatenate([flat, other]), jnp.concatenate([other, flat])
        )
    return flat.astype(jnp.float32)


def depthwise(padded, dw_weight, out_rows, out_cols):
    conv_sum = jnp.zeros((padded.shape[0], out_rows, out_cols), jnp.float32)
    for shift_a in range(KS):
        for shift_b in range(KS):
            tap_weight = dw_weight[:, shift_a * KS + shift_b][:, None, None]
            window = padded[:, shift_a : shift_a + out_rows, shift_b : shift_b + out_cols].astype(
                jnp.float32
            )
            conv_sum = conv_sum + tap_weight * window
    return conv_sum


def depthwise_grad(d_conv, padded, out_rows, out_cols):
    columns = []
    for shift_a in range(KS):
        for shift_b in range(KS):
            window = padded[:, shift_a : shift_a + out_rows, shift_b : shift_b + out_cols].astype(
                jnp.float32
            )
            columns.append(jnp.sum(d_conv * window, axis=(1, 2)))
    return jnp.stack(columns, axis=1)


def cell_pass(conv_blk, state_blk, cot_blk, mask_blk, norm_gain, expand_weight, reduce_weight):
    chan_mean = jnp.mean(conv_blk, axis=0, keepdims=True)
    centred = conv_blk - chan_mean
    chan_var = jnp.mean(centred * centred, axis=0, keepdims=True)
    inv_std = lax.rsqrt(chan_var + norm_eps)
    normed = centred * inv_std
    scaled = (normed * norm_gain[:, None]).astype(jnp.bfloat16)
    pre_act = jnp.dot(expand_weight.T, scaled, preferred_element_type=jnp.float32)
    normal_cdf = 0.5 * (1.0 + lax.erf(pre_act * root_half))
    normal_pdf = jnp.exp(-0.5 * pre_act * pre_act) * gauss_norm
    hidden = (pre_act * normal_cdf).astype(jnp.bfloat16)
    gelu_slope = normal_cdf + pre_act * normal_pdf
    branch = jnp.dot(reduce_weight.T, hidden, preferred_element_type=jnp.float32)
    out_blk = ((state_blk.astype(jnp.float32) + branch) * mask_blk[None, :]).astype(jnp.bfloat16)
    grad_reduce = jnp.dot(hidden, cot_blk.T, preferred_element_type=jnp.float32)
    d_hidden = jnp.dot(reduce_weight, cot_blk, preferred_element_type=jnp.float32)
    d_pre = (d_hidden * gelu_slope).astype(jnp.bfloat16)
    grad_expand = jnp.dot(scaled, d_pre.T, preferred_element_type=jnp.float32)
    d_scaled = jnp.dot(expand_weight, d_pre, preferred_element_type=jnp.float32)
    grad_gain = jnp.sum(d_scaled * normed, axis=1)
    d_normed = d_scaled * norm_gain[:, None]
    d_conv = inv_std * (
        d_normed
        - jnp.mean(d_normed, axis=0, keepdims=True)
        - normed * jnp.mean(d_normed * normed, axis=0, keepdims=True)
    )
    return (out_blk, d_conv, grad_expand, grad_reduce, grad_gain)


def body(ocean_state, ocean_mask, dw_weight, norm_gain, expand_weight, reduce_weight, cotangent):
    state_tile = ocean_state[0]
    channels = state_tile.shape[0]
    tile_rows = state_tile.shape[1]
    tile_cols = state_tile.shape[2]
    margin = KS // 2
    mask_bf = ocean_mask.astype(jnp.bfloat16)
    masked = state_tile * mask_bf[None]
    padded = with_halo(masked, (("lon", 2), ("lat", 1)), margin)
    lat_now = lax.axis_index("lat")
    lat_count = lax.axis_size("lat")
    lon_count = lax.axis_size("lon")
    top_strip = padded[:, tile_rows : tile_rows + margin, :][:, ::-1, ::-1]
    mirrored = mirrored_across(top_strip, "lon")
    north_rows = jnp.where(lat_now == lat_count - 1, mirrored, padded[:, tile_rows + margin :, :])
    south_rows = jnp.where(lat_now == 0, jnp.zeros_like(top_strip), padded[:, :margin, :])
    padded = jnp.concatenate(
        [south_rows, padded[:, margin : tile_rows + margin, :], north_rows], axis=1
    )
    conv_out = depthwise(padded, dw_weight, tile_rows, tile_cols)
    cell_count = tile_rows * tile_cols
    cot_masked = (cotangent[0] * mask_bf[None]).reshape(channels, cell_count)
    out_flat, d_conv, grad_expand, grad_reduce, grad_gain = cell_pass(
        conv_out.reshape(channels, cell_count),
        state_tile.reshape(channels, cell_count),
        cot_masked,
        ocean_mask.astype(jnp.float32).reshape(cell_count),
        norm_gain,
        expand_weight,
        reduce_weight,
    )
    grad_depthwise = depthwise_grad(
        d_conv.reshape(channels, tile_rows, tile_cols), padded, tile_rows, tile_cols
    )
    grad_scale = 1.0 / math.sqrt(lax.axis_size("ens") * lat_count * lon_count * cell_count)
    grad_expand = grad_expand * grad_scale
    grad_reduce = grad_reduce * grad_scale
    grad_gain = grad_gain * grad_scale
    grad_depthwise = grad_depthwise * grad_scale
    width = grad_expand.shape[1]
    small = jnp.concatenate([grad_depthwise, grad_gain[:, None]], axis=1).reshape(-1)
    small_rows = -(-small.shape[0] // width)
    small_rows += -small_rows % 8
    small = jnp.pad(small, (0, small_rows * width - small.shape[0])).reshape(small_rows, width)
    packed = jnp.concatenate([grad_expand, grad_reduce.T, small], axis=0)
    steps = list(REDUCE_ORDER)
    for bit in range(lax.axis_size("lon").bit_length() - 1):
        if ("lon", bit) not in steps:
            steps.append(("lon", bit))
    packed = tree_psum(packed, steps, jnp.float32)
    grad_expand = packed[:channels]
    grad_reduce = packed[channels : 2 * channels].T
    small = packed[2 * channels :].reshape(-1)[: channels * (KS * KS + 1)].reshape(channels, -1)
    grad_depthwise = small[:, : KS * KS]
    grad_gain = small[:, KS * KS]
    next_state = out_flat.reshape(channels, tile_rows, tile_cols)[None]
    return (next_state, grad_depthwise, grad_gain, grad_expand, grad_reduce)


def solution(mesh):
    return jax.shard_map(
        body,
        mesh=mesh,
        in_specs=(
            P("ens", None, "lat", "lon"),
            P("lat", "lon"),
            P(),
            P(),
            P(),
            P(),
            P("ens", None, "lat", "lon"),
        ),
        out_specs=(P("ens", None, "lat", "lon"), P(), P(), P(), P()),
        check_vma=False,
    )
```

```python
import math

import jax
import jax.numpy as jnp
from jax import lax
from jax.sharding import PartitionSpec as P

KS = 7


norm_eps = 1e-06
root_half = 0.7071067811865476
gauss_norm = 0.3989422804014327


def with_halo(cells, sides, width):
    for axis, dim in sides:
        count = lax.axis_size(axis)
        head = lax.slice_in_dim(cells, 0, width, axis=dim)
        tail = lax.slice_in_dim(cells, cells.shape[dim] - width, cells.shape[dim], axis=dim)
        cells = jnp.concatenate(
            [
                lax.ppermute(tail, axis, [(i, (i + 1) % count) for i in range(count)]),
                cells,
                lax.ppermute(head, axis, [((i + 1) % count, i) for i in range(count)]),
            ],
            axis=dim,
        )
    return cells


def swapped(array, axis, stride):
    return lax.ppermute(array, axis, [(i, i ^ 1 << stride) for i in range(lax.axis_size(axis))])


def mirrored_across(array, axis):
    count = lax.axis_size(axis)
    return lax.ppermute(array, axis, [(i, count - 1 - i) for i in range(count)])


REDUCE_ORDER = (
    ("lon", 0), ("lat", None), ("ens", None), ("lon", 1), ("lon", 4), ("lon", 2), ("lon", 3),
)


def spread(array, axis):
    count = lax.axis_size(axis)
    copies = jnp.broadcast_to(array[None], (count,) + array.shape)
    return lax.all_to_all(copies, axis, 0, 0, tiled=False)


def tree_psum(flat, steps, gather_dtype):
    scattered = []
    for axis, bit in steps:
        rows = flat.shape[0]
        if bit is None:
            count = lax.axis_size(axis)
            if rows % count == 0:
                chunks = flat.reshape((count, rows // count) + flat.shape[1:])
                flat = lax.all_to_all(chunks, axis, 0, 0, tiled=False).sum(0)
                scattered.append((axis, bit))
            else:
                flat = spread(flat, axis).sum(0)
            continue
        if (1 << bit) >= lax.axis_size(axis):
            continue
        upper = (lax.axis_index(axis) >> bit) & 1
        if rows % 2 == 0 and rows >= 8:
            half = rows // 2
            low, high = flat[:half], flat[half:]
            keep = jnp.where(upper == 0, low, high)
            send = jnp.where(upper == 0, high, low)
            flat = keep + swapped(send, axis, bit)
            scattered.append((axis, bit))
        else:
            flat = flat + swapped(flat, axis, bit)
    flat = flat.astype(gather_dtype)
    for axis, bit in reversed(scattered):
        if bit is None:
            gathered = spread(flat, axis)
            flat = gathered.reshape((-1,) + flat.shape[1:])
            continue
        upper = (lax.axis_index(axis) >> bit) & 1
        other = swapped(flat, axis, bit)
        flat = jnp.where(
            upper == 0, jnp.concatenate([flat, other]), jnp.concatenate([other, flat])
        )
    return flat.astype(jnp.float32)


def depthwise(padded, dw_weight, out_rows, out_cols):
    conv_sum = jnp.zeros((padded.shape[0], out_rows, out_cols), jnp.float32)
    for shift_a in range(KS):
        for shift_b in range(KS):
            tap_weight = dw_weight[:, shift_a * KS + shift_b][:, None, None]
            window = padded[:, shift_a : shift_a + out_rows, shift_b : shift_b + out_cols].astype(
                jnp.float32
            )
            conv_sum = conv_sum + tap_weight * window
    return conv_sum


def depthwise_grad(d_conv, padded, out_rows, out_cols):
    columns = []
    for shift_a in range(KS):
        for shift_b in range(KS):
            window = padded[:, shift_a : shift_a + out_rows, shift_b : shift_b + out_cols].astype(
                jnp.float32
            )
            columns.append(jnp.sum(d_conv * window, axis=(1, 2)))
    return jnp.stack(columns, axis=0)


def cell_pass(conv_blk, state_blk, cot_blk, mask_blk, norm_gain, expand_weight, reduce_weight):
    chan_mean = jnp.mean(conv_blk, axis=0, keepdims=True)
    centred = conv_blk - chan_mean
    chan_var = jnp.mean(centred * centred, axis=0, keepdims=True)
    inv_std = lax.rsqrt(chan_var + norm_eps)
    normed = centred * inv_std
    scaled = (normed * norm_gain[:, None]).astype(jnp.bfloat16)
    pre_act = jnp.dot(expand_weight.T, scaled, preferred_element_type=jnp.float32)
    normal_cdf = 0.5 * (1.0 + lax.erf(pre_act * root_half))
    normal_pdf = jnp.exp(-0.5 * pre_act * pre_act) * gauss_norm
    hidden = (pre_act * normal_cdf).astype(jnp.bfloat16)
    gelu_slope = normal_cdf + pre_act * normal_pdf
    branch = jnp.dot(reduce_weight.T, hidden, preferred_element_type=jnp.float32)
    out_blk = ((state_blk.astype(jnp.float32) + branch) * mask_blk[None, :]).astype(jnp.bfloat16)
    grad_reduce = jnp.dot(hidden, cot_blk.T, preferred_element_type=jnp.float32)
    d_hidden = jnp.dot(reduce_weight, cot_blk, preferred_element_type=jnp.float32)
    d_pre = (d_hidden * gelu_slope).astype(jnp.bfloat16)
    grad_expand = jnp.dot(scaled, d_pre.T, preferred_element_type=jnp.float32)
    d_scaled = jnp.dot(expand_weight, d_pre, preferred_element_type=jnp.float32)
    grad_gain = jnp.sum(d_scaled * normed, axis=1)
    d_normed = d_scaled * norm_gain[:, None]
    d_conv = inv_std * (
        d_normed
        - jnp.mean(d_normed, axis=0, keepdims=True)
        - normed * jnp.mean(d_normed * normed, axis=0, keepdims=True)
    )
    return (out_blk, d_conv, grad_expand, grad_reduce, grad_gain)


def body(ocean_state, ocean_mask, dw_weight, norm_gain, expand_weight, reduce_weight, cotangent):
    state_tile = ocean_state[0]
    channels = state_tile.shape[0]
    tile_rows = state_tile.shape[1]
    tile_cols = state_tile.shape[2]
    margin = KS // 2
    mask_bf = ocean_mask.astype(jnp.bfloat16)
    masked = state_tile * mask_bf[None]
    padded = with_halo(masked, (("lon", 2), ("lat", 1)), margin)
    lat_now = lax.axis_index("lat")
    lat_count = lax.axis_size("lat")
    lon_count = lax.axis_size("lon")
    top_strip = padded[:, tile_rows : tile_rows + margin, :][:, ::-1, ::-1]
    mirrored = mirrored_across(top_strip, "lon")
    north_rows = jnp.where(lat_now == lat_count - 1, mirrored, padded[:, tile_rows + margin :, :])
    south_rows = jnp.where(lat_now == 0, jnp.zeros_like(top_strip), padded[:, :margin, :])
    padded = jnp.concatenate(
        [south_rows, padded[:, margin : tile_rows + margin, :], north_rows], axis=1
    )
    conv_out = depthwise(padded, dw_weight, tile_rows, tile_cols)
    cell_count = tile_rows * tile_cols
    cot_masked = (cotangent[0] * mask_bf[None]).reshape(channels, cell_count)
    out_flat, d_conv, grad_expand, grad_reduce, grad_gain = cell_pass(
        conv_out.reshape(channels, cell_count),
        state_tile.reshape(channels, cell_count),
        cot_masked,
        ocean_mask.astype(jnp.float32).reshape(cell_count),
        norm_gain,
        expand_weight,
        reduce_weight,
    )
    grad_depthwise = depthwise_grad(
        d_conv.reshape(channels, tile_rows, tile_cols), padded, tile_rows, tile_cols
    )
    grad_scale = 1.0 / math.sqrt(lax.axis_size("ens") * lat_count * lon_count * cell_count)
    grad_expand = grad_expand * grad_scale
    grad_reduce = grad_reduce * grad_scale
    grad_gain = grad_gain * grad_scale
    grad_depthwise = grad_depthwise * grad_scale
    width = grad_expand.shape[1]
    small = jnp.concatenate([grad_depthwise, grad_gain[None]], axis=0).reshape(-1)
    small_rows = -(-small.shape[0] // width)
    small_rows += -small_rows % 8
    small = jnp.pad(small, (0, small_rows * width - small.shape[0])).reshape(small_rows, width)
    packed = jnp.concatenate([grad_expand, grad_reduce.T, small], axis=0)
    steps = list(REDUCE_ORDER)
    for bit in range(lax.axis_size("lon").bit_length() - 1):
        if ("lon", bit) not in steps:
            steps.append(("lon", bit))
    packed = tree_psum(packed, steps, jnp.float32)
    grad_expand = packed[:channels]
    grad_reduce = packed[channels : 2 * channels].T
    small = packed[2 * channels :].reshape(-1)[: channels * (KS * KS + 1)].reshape(-1, channels)
    grad_depthwise = small[: KS * KS].T
    grad_gain = small[KS * KS]
    next_state = out_flat.reshape(channels, tile_rows, tile_cols)[None]
    return (next_state, grad_depthwise, grad_gain, grad_expand, grad_reduce)


def solution(mesh):
    return jax.shard_map(
        body,
        mesh=mesh,
        in_specs=(
            P("ens", None, "lat", "lon"),
            P("lat", "lon"),
            P(),
            P(),
            P(),
            P(),
            P("ens", None, "lat", "lon"),
        ),
        out_specs=(P("ens", None, "lat", "lon"), P(), P(), P(), P()),
        check_vma=False,
    )
```

```python
import math

import jax
import jax.numpy as jnp
from jax import lax
from jax.sharding import Mesh, PartitionSpec as P

KS = 7


norm_eps = 1e-06
root_half = 0.7071067811865476
gauss_norm = 0.3989422804014327


def with_halo(cells, sides, width):
    for axis, dim in sides:
        count = lax.axis_size(axis)
        head = lax.slice_in_dim(cells, 0, width, axis=dim)
        tail = lax.slice_in_dim(cells, cells.shape[dim] - width, cells.shape[dim], axis=dim)
        cells = jnp.concatenate(
            [
                lax.ppermute(tail, axis, [(i, (i + 1) % count) for i in range(count)]),
                cells,
                lax.ppermute(head, axis, [((i + 1) % count, i) for i in range(count)]),
            ],
            axis=dim,
        )
    return cells


def swapped(array, axis, stride):
    return lax.ppermute(array, axis, [(i, i ^ 1 << stride) for i in range(lax.axis_size(axis))])


def mirrored_across(array, axis):
    count = lax.axis_size(axis)
    return lax.ppermute(array, axis, [(i, count - 1 - i) for i in range(count)])


LON = ("lon_z", "lon_y", "lon_c")
REDUCE_ORDER = (("lon_c", 0), ("lat", None), ("ens", None), ("lon_y", None), ("lon_z", 0))


def spread(array, axis):
    count = lax.axis_size(axis)
    copies = jnp.broadcast_to(array[None], (count,) + array.shape)
    return lax.all_to_all(copies, axis, 0, 0, tiled=False)


def tree_psum(flat, steps, gather_dtype):
    scattered = []
    for axis, bit in steps:
        rows = flat.shape[0]
        if bit is None:
            count = lax.axis_size(axis)
            if rows % count == 0:
                chunks = flat.reshape((count, rows // count) + flat.shape[1:])
                flat = lax.all_to_all(chunks, axis, 0, 0, tiled=False).sum(0)
                scattered.append((axis, bit))
            else:
                flat = spread(flat, axis).sum(0)
            continue
        if (1 << bit) >= lax.axis_size(axis):
            continue
        upper = (lax.axis_index(axis) >> bit) & 1
        if rows % 2 == 0 and rows >= 8:
            half = rows // 2
            low, high = flat[:half], flat[half:]
            keep = jnp.where(upper == 0, low, high)
            send = jnp.where(upper == 0, high, low)
            flat = keep + swapped(send, axis, bit)
            scattered.append((axis, bit))
        else:
            flat = flat + swapped(flat, axis, bit)
    flat = flat.astype(gather_dtype)
    for axis, bit in reversed(scattered):
        if bit is None:
            gathered = spread(flat, axis)
            flat = gathered.reshape((-1,) + flat.shape[1:])
            continue
        upper = (lax.axis_index(axis) >> bit) & 1
        other = swapped(flat, axis, bit)
        flat = jnp.where(
            upper == 0, jnp.concatenate([flat, other]), jnp.concatenate([other, flat])
        )
    return flat.astype(jnp.float32)


def depthwise(padded, dw_weight, out_rows, out_cols):
    conv_sum = jnp.zeros((padded.shape[0], out_rows, out_cols), jnp.float32)
    for shift_a in range(KS):
        for shift_b in range(KS):
            tap_weight = dw_weight[:, shift_a * KS + shift_b][:, None, None]
            window = padded[:, shift_a : shift_a + out_rows, shift_b : shift_b + out_cols].astype(
                jnp.float32
            )
            conv_sum = conv_sum + tap_weight * window
    return conv_sum


def depthwise_grad(d_conv, padded, out_rows, out_cols):
    columns = []
    for shift_a in range(KS):
        for shift_b in range(KS):
            window = padded[:, shift_a : shift_a + out_rows, shift_b : shift_b + out_cols].astype(
                jnp.float32
            )
            columns.append(jnp.sum(d_conv * window, axis=(1, 2)))
    return jnp.stack(columns, axis=0)


def cell_pass(conv_blk, state_blk, cot_blk, mask_blk, norm_gain, expand_weight, reduce_weight):
    chan_mean = jnp.mean(conv_blk, axis=0, keepdims=True)
    centred = conv_blk - chan_mean
    chan_var = jnp.mean(centred * centred, axis=0, keepdims=True)
    inv_std = lax.rsqrt(chan_var + norm_eps)
    normed = centred * inv_std
    scaled = (normed * norm_gain[:, None]).astype(jnp.bfloat16)
    pre_act = jnp.dot(expand_weight.T, scaled, preferred_element_type=jnp.float32)
    normal_cdf = 0.5 * (1.0 + lax.erf(pre_act * root_half))
    normal_pdf = jnp.exp(-0.5 * pre_act * pre_act) * gauss_norm
    hidden = (pre_act * normal_cdf).astype(jnp.bfloat16)
    gelu_slope = normal_cdf + pre_act * normal_pdf
    branch = jnp.dot(reduce_weight.T, hidden, preferred_element_type=jnp.float32)
    out_blk = ((state_blk.astype(jnp.float32) + branch) * mask_blk[None, :]).astype(jnp.bfloat16)
    grad_reduce = jnp.dot(hidden, cot_blk.T, preferred_element_type=jnp.float32)
    d_hidden = jnp.dot(reduce_weight, cot_blk, preferred_element_type=jnp.float32)
    d_pre = (d_hidden * gelu_slope).astype(jnp.bfloat16)
    grad_expand = jnp.dot(scaled, d_pre.T, preferred_element_type=jnp.float32)
    d_scaled = jnp.dot(expand_weight, d_pre, preferred_element_type=jnp.float32)
    grad_gain = jnp.sum(d_scaled * normed, axis=1)
    d_normed = d_scaled * norm_gain[:, None]
    d_conv = inv_std * (
        d_normed
        - jnp.mean(d_normed, axis=0, keepdims=True)
        - normed * jnp.mean(d_normed * normed, axis=0, keepdims=True)
    )
    return (out_blk, d_conv, grad_expand, grad_reduce, grad_gain)


def body(ocean_state, ocean_mask, dw_weight, norm_gain, expand_weight, reduce_weight, cotangent):
    state_tile = ocean_state[0]
    channels = state_tile.shape[0]
    tile_rows = state_tile.shape[1]
    tile_cols = state_tile.shape[2]
    margin = KS // 2
    mask_bf = ocean_mask.astype(jnp.bfloat16)
    masked = state_tile * mask_bf[None]
    padded = with_halo(masked, ((LON, 2), ("lat", 1)), margin)
    lat_now = lax.axis_index("lat")
    lat_count = lax.axis_size("lat")
    lon_count = lax.axis_size(LON)
    top_strip = padded[:, tile_rows : tile_rows + margin, :][:, ::-1, ::-1]
    mirrored = mirrored_across(top_strip, LON)
    north_rows = jnp.where(lat_now == lat_count - 1, mirrored, padded[:, tile_rows + margin :, :])
    south_rows = jnp.where(lat_now == 0, jnp.zeros_like(top_strip), padded[:, :margin, :])
    padded = jnp.concatenate(
        [south_rows, padded[:, margin : tile_rows + margin, :], north_rows], axis=1
    )
    conv_out = depthwise(padded, dw_weight, tile_rows, tile_cols)
    cell_count = tile_rows * tile_cols
    cot_masked = (cotangent[0] * mask_bf[None]).reshape(channels, cell_count)
    out_flat, d_conv, grad_expand, grad_reduce, grad_gain = cell_pass(
        conv_out.reshape(channels, cell_count),
        state_tile.reshape(channels, cell_count),
        cot_masked,
        ocean_mask.astype(jnp.float32).reshape(cell_count),
        norm_gain,
        expand_weight,
        reduce_weight,
    )
    grad_depthwise = depthwise_grad(
        d_conv.reshape(channels, tile_rows, tile_cols), padded, tile_rows, tile_cols
    )
    grad_scale = 1.0 / math.sqrt(lax.axis_size("ens") * lat_count * lon_count * cell_count)
    grad_expand = grad_expand * grad_scale
    grad_reduce = grad_reduce * grad_scale
    grad_gain = grad_gain * grad_scale
    grad_depthwise = grad_depthwise * grad_scale
    width = grad_expand.shape[1]
    small = jnp.concatenate([grad_depthwise, grad_gain[None]], axis=0).reshape(-1)
    small_rows = -(-small.shape[0] // width)
    small_rows += -small_rows % 8
    small = jnp.pad(small, (0, small_rows * width - small.shape[0])).reshape(small_rows, width)
    packed = jnp.concatenate([grad_expand, grad_reduce.T, small], axis=0)
    packed = tree_psum(packed, REDUCE_ORDER, jnp.float32)
    grad_expand = packed[:channels]
    grad_reduce = packed[channels : 2 * channels].T
    small = packed[2 * channels :].reshape(-1)[: channels * (KS * KS + 1)].reshape(-1, channels)
    grad_depthwise = small[: KS * KS].T
    grad_gain = small[KS * KS]
    next_state = out_flat.reshape(channels, tile_rows, tile_cols)[None]
    return (next_state, grad_depthwise, grad_gain, grad_expand, grad_reduce)


def solution(mesh):
    ens, lon, lat = (mesh.shape[name] for name in ("ens", "lon", "lat"))
    fine = Mesh(mesh.devices.reshape(ens, 2, lon // 4, 2, lat), ("ens",) + LON + ("lat",))
    return jax.shard_map(
        body,
        mesh=fine,
        in_specs=(
            P("ens", None, "lat", LON),
            P("lat", LON),
            P(),
            P(),
            P(),
            P(),
            P("ens", None, "lat", LON),
        ),
        out_specs=(P("ens", None, "lat", LON), P(), P(), P(), P()),
        check_vma=False,
    )
```

```python
import math

import jax
import jax.numpy as jnp
from jax import lax
from jax.sharding import Mesh, PartitionSpec as P

KS = 7


norm_eps = 1e-06
root_half = 0.7071067811865476
gauss_norm = 0.3989422804014327


def with_halo(cells, sides, width):
    for axis, dim in sides:
        count = lax.axis_size(axis)
        head = lax.slice_in_dim(cells, 0, width, axis=dim)
        tail = lax.slice_in_dim(cells, cells.shape[dim] - width, cells.shape[dim], axis=dim)
        cells = jnp.concatenate(
            [
                lax.ppermute(tail, axis, [(i, (i + 1) % count) for i in range(count)]),
                cells,
                lax.ppermute(head, axis, [((i + 1) % count, i) for i in range(count)]),
            ],
            axis=dim,
        )
    return cells


def swapped(array, axis, stride):
    return lax.ppermute(array, axis, [(i, i ^ 1 << stride) for i in range(lax.axis_size(axis))])


def mirrored_across(array, axis):
    count = lax.axis_size(axis)
    return lax.ppermute(array, axis, [(i, count - 1 - i) for i in range(count)])


LON = ("lon_z", "lon_y", "lon_c")
REDUCE_ORDER = (("lon_c", 0), ("lat", None), ("ens", None), ("lon_y", None), ("lon_z", 0))


def spread(array, axis):
    count = lax.axis_size(axis)
    copies = jnp.broadcast_to(array[None], (count,) + array.shape)
    return lax.all_to_all(copies, axis, 0, 0, tiled=False)


def tree_psum(flat, steps, gather_dtype):
    scattered = []
    for axis, bit in steps:
        rows = flat.shape[0]
        if bit is None:
            count = lax.axis_size(axis)
            if rows % count == 0:
                chunks = flat.reshape((count, rows // count) + flat.shape[1:])
                flat = lax.all_to_all(chunks, axis, 0, 0, tiled=False).sum(0)
                scattered.append((axis, bit))
            else:
                flat = spread(flat, axis).sum(0)
            continue
        if (1 << bit) >= lax.axis_size(axis):
            continue
        upper = (lax.axis_index(axis) >> bit) & 1
        if rows % 2 == 0 and rows >= 8:
            half = rows // 2
            low, high = flat[:half], flat[half:]
            keep = jnp.where(upper == 0, low, high)
            send = jnp.where(upper == 0, high, low)
            flat = keep + swapped(send, axis, bit)
            scattered.append((axis, bit))
        else:
            flat = flat + swapped(flat, axis, bit)
    flat = flat.astype(gather_dtype)
    for axis, bit in reversed(scattered):
        if bit is None:
            gathered = spread(flat, axis)
            flat = gathered.reshape((-1,) + flat.shape[1:])
            continue
        upper = (lax.axis_index(axis) >> bit) & 1
        other = swapped(flat, axis, bit)
        flat = jnp.where(
            upper == 0, jnp.concatenate([flat, other]), jnp.concatenate([other, flat])
        )
    return flat.astype(jnp.float32)


def depthwise(padded, dw_weight, out_rows, out_cols):
    conv_sum = jnp.zeros((padded.shape[0], out_rows, out_cols), jnp.float32)
    for shift_a in range(KS):
        for shift_b in range(KS):
            tap_weight = dw_weight[:, shift_a * KS + shift_b][:, None, None]
            window = padded[:, shift_a : shift_a + out_rows, shift_b : shift_b + out_cols].astype(
                jnp.float32
            )
            conv_sum = conv_sum + tap_weight * window
    return conv_sum


def depthwise_grad(d_conv, padded, out_rows, out_cols):
    columns = []
    for shift_a in range(KS):
        for shift_b in range(KS):
            window = padded[:, shift_a : shift_a + out_rows, shift_b : shift_b + out_cols].astype(
                jnp.float32
            )
            columns.append(jnp.sum(d_conv * window, axis=(1, 2)))
    return jnp.stack(columns, axis=0)


def cell_pass(conv_blk, state_blk, cot_blk, mask_blk, norm_gain, expand_weight, reduce_weight):
    chan_mean = jnp.mean(conv_blk, axis=0, keepdims=True)
    centred = conv_blk - chan_mean
    chan_var = jnp.mean(centred * centred, axis=0, keepdims=True)
    inv_std = lax.rsqrt(chan_var + norm_eps)
    normed = centred * inv_std
    scaled = (normed * norm_gain[:, None]).astype(jnp.bfloat16)
    pre_act = jnp.dot(expand_weight.T, scaled, preferred_element_type=jnp.float32)
    normal_cdf = 0.5 * (1.0 + lax.erf(pre_act * root_half))
    normal_pdf = jnp.exp(-0.5 * pre_act * pre_act) * gauss_norm
    hidden = (pre_act * normal_cdf).astype(jnp.bfloat16)
    gelu_slope = normal_cdf + pre_act * normal_pdf
    branch = jnp.dot(reduce_weight.T, hidden, preferred_element_type=jnp.float32)
    out_blk = ((state_blk.astype(jnp.float32) + branch) * mask_blk[None, :]).astype(jnp.bfloat16)
    grad_reduce = jnp.dot(hidden, cot_blk.T, preferred_element_type=jnp.float32)
    d_hidden = jnp.dot(reduce_weight, cot_blk, preferred_element_type=jnp.float32)
    d_pre = (d_hidden * gelu_slope).astype(jnp.bfloat16)
    grad_expand = jnp.dot(scaled, d_pre.T, preferred_element_type=jnp.float32)
    d_scaled = jnp.dot(expand_weight, d_pre, preferred_element_type=jnp.float32)
    grad_gain = jnp.sum(d_scaled * normed, axis=1)
    d_normed = d_scaled * norm_gain[:, None]
    d_conv = inv_std * (
        d_normed
        - jnp.mean(d_normed, axis=0, keepdims=True)
        - normed * jnp.mean(d_normed * normed, axis=0, keepdims=True)
    )
    return (out_blk, d_conv, grad_expand, grad_reduce, grad_gain)


def body(ocean_state, ocean_mask, dw_weight, norm_gain, expand_weight, reduce_weight, cotangent):
    state_tile = ocean_state[0]
    channels = state_tile.shape[0]
    tile_rows = state_tile.shape[1]
    tile_cols = state_tile.shape[2]
    margin = KS // 2
    mask_bf = ocean_mask.astype(jnp.bfloat16)
    masked = state_tile * mask_bf[None]
    padded = with_halo(masked, ((LON, 2), ("lat", 1)), margin)
    lat_now = lax.axis_index("lat")
    lat_count = lax.axis_size("lat")
    lon_count = lax.axis_size(LON)
    top_strip = padded[:, tile_rows : tile_rows + margin, :][:, ::-1, ::-1]
    mirrored = mirrored_across(top_strip, LON)
    north_rows = jnp.where(lat_now == lat_count - 1, mirrored, padded[:, tile_rows + margin :, :])
    south_rows = jnp.where(lat_now == 0, jnp.zeros_like(top_strip), padded[:, :margin, :])
    padded = jnp.concatenate(
        [south_rows, padded[:, margin : tile_rows + margin, :], north_rows], axis=1
    )
    conv_out = depthwise(padded, dw_weight, tile_rows, tile_cols)
    cell_count = tile_rows * tile_cols
    cot_masked = (cotangent[0] * mask_bf[None]).reshape(channels, cell_count)
    out_flat, d_conv, grad_expand, grad_reduce, grad_gain = cell_pass(
        conv_out.reshape(channels, cell_count),
        state_tile.reshape(channels, cell_count),
        cot_masked,
        ocean_mask.astype(jnp.float32).reshape(cell_count),
        norm_gain,
        expand_weight,
        reduce_weight,
    )
    grad_depthwise = depthwise_grad(
        d_conv.reshape(channels, tile_rows, tile_cols), padded, tile_rows, tile_cols
    )
    grad_scale = 1.0 / math.sqrt(lax.axis_size("ens") * lat_count * lon_count * cell_count)
    grad_expand = grad_expand * grad_scale
    grad_reduce = grad_reduce * grad_scale
    grad_gain = grad_gain * grad_scale
    grad_depthwise = grad_depthwise * grad_scale
    width = grad_expand.shape[1]
    small = jnp.concatenate([grad_depthwise, grad_gain[None]], axis=0).reshape(-1)
    small_rows = -(-small.shape[0] // width)
    small_rows += -small_rows % 8
    small = jnp.pad(small, (0, small_rows * width - small.shape[0])).reshape(small_rows, width)
    packed = jnp.concatenate([grad_expand, grad_reduce.T, small], axis=0)
    packed = tree_psum(packed, REDUCE_ORDER, jnp.bfloat16)
    grad_expand = packed[:channels]
    grad_reduce = packed[channels : 2 * channels].T
    small = packed[2 * channels :].reshape(-1)[: channels * (KS * KS + 1)].reshape(-1, channels)
    grad_depthwise = small[: KS * KS].T
    grad_gain = small[KS * KS]
    next_state = out_flat.reshape(channels, tile_rows, tile_cols)[None]
    return (next_state, grad_depthwise, grad_gain, grad_expand, grad_reduce)


def solution(mesh):
    ens, lon, lat = (mesh.shape[name] for name in ("ens", "lon", "lat"))
    fine = Mesh(mesh.devices.reshape(ens, 2, lon // 4, 2, lat), ("ens",) + LON + ("lat",))
    return jax.shard_map(
        body,
        mesh=fine,
        in_specs=(
            P("ens", None, "lat", LON),
            P("lat", LON),
            P(),
            P(),
            P(),
            P(),
            P("ens", None, "lat", LON),
        ),
        out_specs=(P("ens", None, "lat", LON), P(), P(), P(), P()),
        check_vma=False,
    )
```

```python
import math

import jax
import jax.numpy as jnp
from jax import lax
from jax.sharding import Mesh, PartitionSpec as P

KS = 7


norm_eps = 1e-06
root_half = 0.7071067811865476
gauss_norm = 0.3989422804014327


def with_halo(cells, sides, width):
    for axis, dim in sides:
        count = lax.axis_size(axis)
        head = lax.slice_in_dim(cells, 0, width, axis=dim)
        tail = lax.slice_in_dim(cells, cells.shape[dim] - width, cells.shape[dim], axis=dim)
        cells = jnp.concatenate(
            [
                lax.ppermute(tail, axis, [(i, (i + 1) % count) for i in range(count)]),
                cells,
                lax.ppermute(head, axis, [((i + 1) % count, i) for i in range(count)]),
            ],
            axis=dim,
        )
    return cells


def swapped(array, axis, stride):
    return lax.ppermute(array, axis, [(i, i ^ 1 << stride) for i in range(lax.axis_size(axis))])


def mirrored_across(array, axis):
    count = lax.axis_size(axis)
    return lax.ppermute(array, axis, [(i, count - 1 - i) for i in range(count)])


LON = ("lon_z", "lon_y", "lon_c")
REDUCE_ORDER = (("lon_c", 0), ("lat", None), ("ens", None), ("lon_z", 0), ("lon_y", None))


def spread(array, axis):
    count = lax.axis_size(axis)
    copies = jnp.broadcast_to(array[None], (count,) + array.shape)
    return lax.all_to_all(copies, axis, 0, 0, tiled=False)


def tree_psum(flat, steps, gather_dtype):
    scattered = []
    for axis, bit in steps:
        rows = flat.shape[0]
        if bit is None:
            count = lax.axis_size(axis)
            if rows % count == 0:
                chunks = flat.reshape((count, rows // count) + flat.shape[1:])
                flat = lax.all_to_all(chunks, axis, 0, 0, tiled=False).sum(0)
                scattered.append((axis, bit))
            else:
                flat = spread(flat, axis).sum(0)
            continue
        if (1 << bit) >= lax.axis_size(axis):
            continue
        upper = (lax.axis_index(axis) >> bit) & 1
        if rows % 2 == 0 and rows >= 8:
            half = rows // 2
            low, high = flat[:half], flat[half:]
            keep = jnp.where(upper == 0, low, high)
            send = jnp.where(upper == 0, high, low)
            flat = keep + swapped(send, axis, bit)
            scattered.append((axis, bit))
        else:
            flat = flat + swapped(flat, axis, bit)
    flat = flat.astype(gather_dtype)
    for axis, bit in reversed(scattered):
        if bit is None:
            gathered = spread(flat, axis)
            flat = gathered.reshape((-1,) + flat.shape[1:])
            continue
        upper = (lax.axis_index(axis) >> bit) & 1
        other = swapped(flat, axis, bit)
        flat = jnp.where(
            upper == 0, jnp.concatenate([flat, other]), jnp.concatenate([other, flat])
        )
    return flat.astype(jnp.float32)


def depthwise(padded, dw_weight, out_rows, out_cols):
    conv_sum = jnp.zeros((padded.shape[0], out_rows, out_cols), jnp.float32)
    for shift_a in range(KS):
        for shift_b in range(KS):
            tap_weight = dw_weight[:, shift_a * KS + shift_b][:, None, None]
            window = padded[:, shift_a : shift_a + out_rows, shift_b : shift_b + out_cols].astype(
                jnp.float32
            )
            conv_sum = conv_sum + tap_weight * window
    return conv_sum


def depthwise_grad(d_conv, padded, out_rows, out_cols):
    columns = []
    for shift_a in range(KS):
        for shift_b in range(KS):
            window = padded[:, shift_a : shift_a + out_rows, shift_b : shift_b + out_cols].astype(
                jnp.float32
            )
            columns.append(jnp.sum(d_conv * window, axis=(1, 2)))
    return jnp.stack(columns, axis=0)


def cell_pass(conv_blk, state_blk, cot_blk, mask_blk, norm_gain, expand_weight, reduce_weight):
    chan_mean = jnp.mean(conv_blk, axis=0, keepdims=True)
    centred = conv_blk - chan_mean
    chan_var = jnp.mean(centred * centred, axis=0, keepdims=True)
    inv_std = lax.rsqrt(chan_var + norm_eps)
    normed = centred * inv_std
    scaled = (normed * norm_gain[:, None]).astype(jnp.bfloat16)
    pre_act = jnp.dot(expand_weight.T, scaled, preferred_element_type=jnp.float32)
    normal_cdf = 0.5 * (1.0 + lax.erf(pre_act * root_half))
    normal_pdf = jnp.exp(-0.5 * pre_act * pre_act) * gauss_norm
    hidden = (pre_act * normal_cdf).astype(jnp.bfloat16)
    gelu_slope = normal_cdf + pre_act * normal_pdf
    branch = jnp.dot(reduce_weight.T, hidden, preferred_element_type=jnp.float32)
    out_blk = ((state_blk.astype(jnp.float32) + branch) * mask_blk[None, :]).astype(jnp.bfloat16)
    grad_reduce = jnp.dot(hidden, cot_blk.T, preferred_element_type=jnp.float32)
    d_hidden = jnp.dot(reduce_weight, cot_blk, preferred_element_type=jnp.float32)
    d_pre = (d_hidden * gelu_slope).astype(jnp.bfloat16)
    grad_expand = jnp.dot(scaled, d_pre.T, preferred_element_type=jnp.float32)
    d_scaled = jnp.dot(expand_weight, d_pre, preferred_element_type=jnp.float32)
    grad_gain = jnp.sum(d_scaled * normed, axis=1)
    d_normed = d_scaled * norm_gain[:, None]
    d_conv = inv_std * (
        d_normed
        - jnp.mean(d_normed, axis=0, keepdims=True)
        - normed * jnp.mean(d_normed * normed, axis=0, keepdims=True)
    )
    return (out_blk, d_conv, grad_expand, grad_reduce, grad_gain)


def body(ocean_state, ocean_mask, dw_weight, norm_gain, expand_weight, reduce_weight, cotangent):
    state_tile = ocean_state[0]
    channels = state_tile.shape[0]
    tile_rows = state_tile.shape[1]
    tile_cols = state_tile.shape[2]
    margin = KS // 2
    mask_bf = ocean_mask.astype(jnp.bfloat16)
    masked = state_tile * mask_bf[None]
    padded = with_halo(masked, ((LON, 2), ("lat", 1)), margin)
    lat_now = lax.axis_index("lat")
    lat_count = lax.axis_size("lat")
    lon_count = lax.axis_size(LON)
    top_strip = padded[:, tile_rows : tile_rows + margin, :][:, ::-1, ::-1]
    mirrored = mirrored_across(top_strip, LON)
    north_rows = jnp.where(lat_now == lat_count - 1, mirrored, padded[:, tile_rows + margin :, :])
    south_rows = jnp.where(lat_now == 0, jnp.zeros_like(top_strip), padded[:, :margin, :])
    padded = jnp.concatenate(
        [south_rows, padded[:, margin : tile_rows + margin, :], north_rows], axis=1
    )
    conv_out = depthwise(padded, dw_weight, tile_rows, tile_cols)
    cell_count = tile_rows * tile_cols
    cot_masked = (cotangent[0] * mask_bf[None]).reshape(channels, cell_count)
    out_flat, d_conv, grad_expand, grad_reduce, grad_gain = cell_pass(
        conv_out.reshape(channels, cell_count),
        state_tile.reshape(channels, cell_count),
        cot_masked,
        ocean_mask.astype(jnp.float32).reshape(cell_count),
        norm_gain,
        expand_weight,
        reduce_weight,
    )
    grad_depthwise = depthwise_grad(
        d_conv.reshape(channels, tile_rows, tile_cols), padded, tile_rows, tile_cols
    )
    grad_scale = 1.0 / math.sqrt(lax.axis_size("ens") * lat_count * lon_count * cell_count)
    grad_expand = grad_expand * grad_scale
    grad_reduce = grad_reduce * grad_scale
    grad_gain = grad_gain * grad_scale
    grad_depthwise = grad_depthwise * grad_scale
    width = grad_expand.shape[1]
    small = jnp.concatenate([grad_depthwise, grad_gain[None]], axis=0).reshape(-1)
    small_rows = -(-small.shape[0] // width)
    small_rows += -small_rows % 8
    small = jnp.pad(small, (0, small_rows * width - small.shape[0])).reshape(small_rows, width)
    packed = jnp.concatenate([grad_expand, grad_reduce.T, small], axis=0)
    packed = tree_psum(packed, REDUCE_ORDER, jnp.bfloat16)
    grad_expand = packed[:channels]
    grad_reduce = packed[channels : 2 * channels].T
    small = packed[2 * channels :].reshape(-1)[: channels * (KS * KS + 1)].reshape(-1, channels)
    grad_depthwise = small[: KS * KS].T
    grad_gain = small[KS * KS]
    next_state = out_flat.reshape(channels, tile_rows, tile_cols)[None]
    return (next_state, grad_depthwise, grad_gain, grad_expand, grad_reduce)


def solution(mesh):
    ens, lon, lat = (mesh.shape[name] for name in ("ens", "lon", "lat"))
    fine = Mesh(mesh.devices.reshape(ens, 2, lon // 4, 2, lat), ("ens",) + LON + ("lat",))
    return jax.shard_map(
        body,
        mesh=fine,
        in_specs=(
            P("ens", None, "lat", LON),
            P("lat", LON),
            P(),
            P(),
            P(),
            P(),
            P("ens", None, "lat", LON),
        ),
        out_specs=(P("ens", None, "lat", LON), P(), P(), P(), P()),
        check_vma=False,
    )
```

```python
import math

import jax
import jax.numpy as jnp
from jax import lax
from jax.sharding import Mesh, PartitionSpec as P

KS = 7


norm_eps = 1e-06
root_half = 0.7071067811865476
gauss_norm = 0.3989422804014327


def with_halo(cells, sides, width):
    for axis, dim in sides:
        count = lax.axis_size(axis)
        head = lax.slice_in_dim(cells, 0, width, axis=dim)
        tail = lax.slice_in_dim(cells, cells.shape[dim] - width, cells.shape[dim], axis=dim)
        cells = jnp.concatenate(
            [
                lax.ppermute(tail, axis, [(i, (i + 1) % count) for i in range(count)]),
                cells,
                lax.ppermute(head, axis, [((i + 1) % count, i) for i in range(count)]),
            ],
            axis=dim,
        )
    return cells


def swapped(array, axis, stride):
    return lax.ppermute(array, axis, [(i, i ^ 1 << stride) for i in range(lax.axis_size(axis))])


def mirrored_across(array, axis):
    count = lax.axis_size(axis)
    return lax.ppermute(array, axis, [(i, count - 1 - i) for i in range(count)])


LON = ("lon_z", "lon_y", "lon_c")
REDUCE_ORDER = (("lon_c", 0), ("lat", None), ("ens", None), ("lon_z", 0), ("lon_y", None))


def spread(array, axis):
    count = lax.axis_size(axis)
    copies = jnp.broadcast_to(array[None], (count,) + array.shape)
    return lax.all_to_all(copies, axis, 0, 0, tiled=False)


def tree_psum(flat, steps, gather_dtype):
    scattered = []
    for axis, bit in steps:
        rows = flat.shape[0]
        if bit is None:
            count = lax.axis_size(axis)
            if rows % count == 0:
                chunks = flat.reshape((count, rows // count) + flat.shape[1:])
                flat = lax.all_to_all(chunks, axis, 0, 0, tiled=False).sum(0)
                scattered.append((axis, bit))
            else:
                flat = spread(flat, axis).sum(0)
            continue
        if (1 << bit) >= lax.axis_size(axis):
            continue
        upper = (lax.axis_index(axis) >> bit) & 1
        if rows % 2 == 0 and rows >= 8:
            half = rows // 2
            low, high = flat[:half], flat[half:]
            keep = jnp.where(upper == 0, low, high)
            send = jnp.where(upper == 0, high, low)
            flat = keep + swapped(send, axis, bit)
            scattered.append((axis, bit))
        else:
            flat = flat + swapped(flat, axis, bit)
    flat = flat.astype(gather_dtype)
    for axis, bit in reversed(scattered):
        if bit is None:
            gathered = spread(flat, axis)
            flat = gathered.reshape((-1,) + flat.shape[1:])
            continue
        upper = (lax.axis_index(axis) >> bit) & 1
        other = swapped(flat, axis, bit)
        flat = jnp.where(
            upper == 0, jnp.concatenate([flat, other]), jnp.concatenate([other, flat])
        )
    return flat.astype(jnp.float32)


def depthwise(padded, dw_weight, out_rows, out_cols):
    conv_sum = jnp.zeros((padded.shape[0], out_rows, out_cols), jnp.float32)
    for shift_a in range(KS):
        for shift_b in range(KS):
            tap_weight = dw_weight[:, shift_a * KS + shift_b][:, None, None]
            window = padded[:, shift_a : shift_a + out_rows, shift_b : shift_b + out_cols].astype(
                jnp.float32
            )
            conv_sum = conv_sum + tap_weight * window
    return conv_sum


def depthwise_grad(d_conv, padded, out_rows, out_cols):
    columns = []
    for shift_a in range(KS):
        for shift_b in range(KS):
            window = padded[:, shift_a : shift_a + out_rows, shift_b : shift_b + out_cols].astype(
                jnp.float32
            )
            columns.append(jnp.sum(d_conv * window, axis=(1, 2)))
    return jnp.stack(columns, axis=0)


def cell_pass(conv_blk, state_blk, cot_blk, mask_blk, norm_gain, expand_weight, reduce_weight):
    chan_mean = jnp.mean(conv_blk, axis=0, keepdims=True)
    centred = conv_blk - chan_mean
    chan_var = jnp.mean(centred * centred, axis=0, keepdims=True)
    inv_std = lax.rsqrt(chan_var + norm_eps)
    normed = centred * inv_std
    scaled = (normed * norm_gain[:, None]).astype(jnp.bfloat16)
    pre_act = jnp.dot(expand_weight.T, scaled, preferred_element_type=jnp.float32)
    normal_cdf = 0.5 * (1.0 + lax.erf(pre_act * root_half))
    normal_pdf = jnp.exp(-0.5 * pre_act * pre_act) * gauss_norm
    hidden = (pre_act * normal_cdf).astype(jnp.bfloat16)
    gelu_slope = normal_cdf + pre_act * normal_pdf
    branch = jnp.dot(reduce_weight.T, hidden, preferred_element_type=jnp.float32)
    out_blk = ((state_blk.astype(jnp.float32) + branch) * mask_blk[None, :]).astype(jnp.bfloat16)
    grad_reduce = jnp.dot(hidden, cot_blk.T, preferred_element_type=jnp.float32)
    d_hidden = jnp.dot(reduce_weight, cot_blk, preferred_element_type=jnp.float32)
    d_pre = (d_hidden * gelu_slope).astype(jnp.bfloat16)
    grad_expand = jnp.dot(scaled, d_pre.T, preferred_element_type=jnp.float32)
    d_scaled = jnp.dot(expand_weight, d_pre, preferred_element_type=jnp.float32)
    grad_gain = jnp.sum(d_scaled * normed, axis=1)
    d_normed = d_scaled * norm_gain[:, None]
    d_conv = inv_std * (
        d_normed
        - jnp.mean(d_normed, axis=0, keepdims=True)
        - normed * jnp.mean(d_normed * normed, axis=0, keepdims=True)
    )
    return (out_blk, d_conv, grad_expand, grad_reduce, grad_gain)


def body(ocean_state, ocean_mask, dw_weight, norm_gain, expand_weight, reduce_weight, cotangent):
    state_tile = ocean_state[0]
    channels = state_tile.shape[0]
    tile_rows = state_tile.shape[1]
    tile_cols = state_tile.shape[2]
    margin = KS // 2
    mask_bf = ocean_mask.astype(jnp.bfloat16)
    masked = state_tile * mask_bf[None]
    lat_now = lax.axis_index("lat")
    lat_count = lax.axis_size("lat")
    lon_count = lax.axis_size(LON)
    rows_out = with_halo(masked, (("lat", 1),), margin)
    top_strip = masked[:, tile_rows - margin :, :][:, ::-1, ::-1]
    mirrored = mirrored_across(top_strip, LON)
    north_rows = jnp.where(lat_now == lat_count - 1, mirrored, rows_out[:, tile_rows + margin :, :])
    south_rows = jnp.where(lat_now == 0, jnp.zeros_like(top_strip), rows_out[:, :margin, :])
    padded = jnp.concatenate([south_rows, masked, north_rows], axis=1)
    padded = with_halo(padded, ((LON, 2),), margin)
    conv_out = depthwise(padded, dw_weight, tile_rows, tile_cols)
    cell_count = tile_rows * tile_cols
    cot_masked = (cotangent[0] * mask_bf[None]).reshape(channels, cell_count)
    out_flat, d_conv, grad_expand, grad_reduce, grad_gain = cell_pass(
        conv_out.reshape(channels, cell_count),
        state_tile.reshape(channels, cell_count),
        cot_masked,
        ocean_mask.astype(jnp.float32).reshape(cell_count),
        norm_gain,
        expand_weight,
        reduce_weight,
    )
    grad_depthwise = depthwise_grad(
        d_conv.reshape(channels, tile_rows, tile_cols), padded, tile_rows, tile_cols
    )
    grad_scale = 1.0 / math.sqrt(lax.axis_size("ens") * lat_count * lon_count * cell_count)
    grad_expand = grad_expand * grad_scale
    grad_reduce = grad_reduce * grad_scale
    grad_gain = grad_gain * grad_scale
    grad_depthwise = grad_depthwise * grad_scale
    width = grad_expand.shape[1]
    small = jnp.concatenate([grad_depthwise, grad_gain[None]], axis=0).reshape(-1)
    small_rows = -(-small.shape[0] // width)
    small_rows += -small_rows % 8
    small = jnp.pad(small, (0, small_rows * width - small.shape[0])).reshape(small_rows, width)
    packed = jnp.concatenate([grad_expand, grad_reduce.T, small], axis=0)
    packed = tree_psum(packed, REDUCE_ORDER, jnp.bfloat16)
    grad_expand = packed[:channels]
    grad_reduce = packed[channels : 2 * channels].T
    small = packed[2 * channels :].reshape(-1)[: channels * (KS * KS + 1)].reshape(-1, channels)
    grad_depthwise = small[: KS * KS].T
    grad_gain = small[KS * KS]
    next_state = out_flat.reshape(channels, tile_rows, tile_cols)[None]
    return (next_state, grad_depthwise, grad_gain, grad_expand, grad_reduce)


def solution(mesh):
    ens, lon, lat = (mesh.shape[name] for name in ("ens", "lon", "lat"))
    fine = Mesh(mesh.devices.reshape(ens, 2, lon // 4, 2, lat), ("ens",) + LON + ("lat",))
    return jax.shard_map(
        body,
        mesh=fine,
        in_specs=(
            P("ens", None, "lat", LON),
            P("lat", LON),
            P(),
            P(),
            P(),
            P(),
            P("ens", None, "lat", LON),
        ),
        out_specs=(P("ens", None, "lat", LON), P(), P(), P(), P()),
        check_vma=False,
    )
```

```python
import math

import jax
import jax.numpy as jnp
from jax import lax
from jax.sharding import Mesh, PartitionSpec as P

KS = 7


norm_eps = 1e-06
root_half = 0.7071067811865476
gauss_norm = 0.3989422804014327


def with_halo(cells, sides, width):
    for axis, dim in sides:
        count = lax.axis_size(axis)
        head = lax.slice_in_dim(cells, 0, width, axis=dim)
        tail = lax.slice_in_dim(cells, cells.shape[dim] - width, cells.shape[dim], axis=dim)
        cells = jnp.concatenate(
            [
                lax.ppermute(tail, axis, [(i, (i + 1) % count) for i in range(count)]),
                cells,
                lax.ppermute(head, axis, [((i + 1) % count, i) for i in range(count)]),
            ],
            axis=dim,
        )
    return cells


def swapped(array, axis, stride):
    return lax.ppermute(array, axis, [(i, i ^ 1 << stride) for i in range(lax.axis_size(axis))])


def mirrored_across(array, axis):
    count = lax.axis_size(axis)
    return lax.ppermute(array, axis, [(i, count - 1 - i) for i in range(count)])


LON = ("lon_z", "lon_y", "lon_c")
REDUCE_ORDER = (("lon_c", 0), ("lat", None), ("ens", None), ("lon_z", 0), ("lon_y", None))


def spread(array, axis):
    count = lax.axis_size(axis)
    copies = jnp.broadcast_to(array[None], (count,) + array.shape)
    return lax.all_to_all(copies, axis, 0, 0, tiled=False)


def tree_psum(flat, steps, gather_dtype):
    scattered = []
    for axis, bit in steps:
        rows = flat.shape[0]
        if bit is None:
            count = lax.axis_size(axis)
            if rows % count == 0:
                chunks = flat.reshape((count, rows // count) + flat.shape[1:])
                flat = lax.all_to_all(chunks, axis, 0, 0, tiled=False).sum(0)
                scattered.append((axis, bit))
            else:
                flat = spread(flat, axis).sum(0)
            continue
        if (1 << bit) >= lax.axis_size(axis):
            continue
        upper = (lax.axis_index(axis) >> bit) & 1
        if rows % 2 == 0 and rows >= 8:
            half = rows // 2
            low, high = flat[:half], flat[half:]
            keep = jnp.where(upper == 0, low, high)
            send = jnp.where(upper == 0, high, low)
            flat = keep + swapped(send, axis, bit)
            scattered.append((axis, bit))
        else:
            flat = flat + swapped(flat, axis, bit)
    flat = flat.astype(gather_dtype)
    for axis, bit in reversed(scattered):
        if bit is None:
            gathered = spread(flat, axis)
            flat = gathered.reshape((-1,) + flat.shape[1:])
            continue
        upper = (lax.axis_index(axis) >> bit) & 1
        other = swapped(flat, axis, bit)
        flat = jnp.where(
            upper == 0, jnp.concatenate([flat, other]), jnp.concatenate([other, flat])
        )
    return flat


def depthwise(padded, dw_weight, out_rows, out_cols):
    conv_sum = jnp.zeros((padded.shape[0], out_rows, out_cols), jnp.float32)
    for shift_a in range(KS):
        for shift_b in range(KS):
            tap_weight = dw_weight[:, shift_a * KS + shift_b][:, None, None]
            window = padded[:, shift_a : shift_a + out_rows, shift_b : shift_b + out_cols].astype(
                jnp.float32
            )
            conv_sum = conv_sum + tap_weight * window
    return conv_sum


def depthwise_grad(d_conv, padded, out_rows, out_cols):
    columns = []
    for shift_a in range(KS):
        for shift_b in range(KS):
            window = padded[:, shift_a : shift_a + out_rows, shift_b : shift_b + out_cols].astype(
                jnp.float32
            )
            columns.append(jnp.sum(d_conv * window, axis=(1, 2)))
    return jnp.stack(columns, axis=0)


def cell_pass(conv_blk, state_blk, cot_blk, mask_blk, norm_gain, expand_weight, reduce_weight):
    chan_mean = jnp.mean(conv_blk, axis=0, keepdims=True)
    centred = conv_blk - chan_mean
    chan_var = jnp.mean(centred * centred, axis=0, keepdims=True)
    inv_std = lax.rsqrt(chan_var + norm_eps)
    normed = centred * inv_std
    scaled = (normed * norm_gain[:, None]).astype(jnp.bfloat16)
    pre_act = jnp.dot(expand_weight.T, scaled, preferred_element_type=jnp.float32)
    normal_cdf = 0.5 * (1.0 + lax.erf(pre_act * root_half))
    normal_pdf = jnp.exp(-0.5 * pre_act * pre_act) * gauss_norm
    hidden = (pre_act * normal_cdf).astype(jnp.bfloat16)
    gelu_slope = normal_cdf + pre_act * normal_pdf
    branch = jnp.dot(reduce_weight.T, hidden, preferred_element_type=jnp.float32)
    out_blk = ((state_blk.astype(jnp.float32) + branch) * mask_blk[None, :]).astype(jnp.bfloat16)
    grad_reduce = jnp.dot(hidden, cot_blk.T, preferred_element_type=jnp.float32)
    d_hidden = jnp.dot(reduce_weight, cot_blk, preferred_element_type=jnp.float32)
    d_pre = (d_hidden * gelu_slope).astype(jnp.bfloat16)
    grad_expand = jnp.dot(scaled, d_pre.T, preferred_element_type=jnp.float32)
    d_scaled = jnp.dot(expand_weight, d_pre, preferred_element_type=jnp.float32)
    grad_gain = jnp.sum(d_scaled * normed, axis=1)
    d_normed = d_scaled * norm_gain[:, None]
    d_conv = inv_std * (
        d_normed
        - jnp.mean(d_normed, axis=0, keepdims=True)
        - normed * jnp.mean(d_normed * normed, axis=0, keepdims=True)
    )
    return (out_blk, d_conv, grad_expand, grad_reduce, grad_gain)


def body(ocean_state, ocean_mask, dw_weight, norm_gain, expand_weight, reduce_weight, cotangent):
    state_tile = ocean_state[0]
    channels = state_tile.shape[0]
    tile_rows = state_tile.shape[1]
    tile_cols = state_tile.shape[2]
    margin = KS // 2
    mask_bf = ocean_mask.astype(jnp.bfloat16)
    masked = state_tile * mask_bf[None]
    padded = with_halo(masked, ((LON, 2), ("lat", 1)), margin)
    lat_now = lax.axis_index("lat")
    lat_count = lax.axis_size("lat")
    lon_count = lax.axis_size(LON)
    top_strip = padded[:, tile_rows : tile_rows + margin, :][:, ::-1, ::-1]
    mirrored = mirrored_across(top_strip, LON)
    north_rows = jnp.where(lat_now == lat_count - 1, mirrored, padded[:, tile_rows + margin :, :])
    south_rows = jnp.where(lat_now == 0, jnp.zeros_like(top_strip), padded[:, :margin, :])
    padded = jnp.concatenate(
        [south_rows, padded[:, margin : tile_rows + margin, :], north_rows], axis=1
    )
    conv_out = depthwise(padded, dw_weight, tile_rows, tile_cols)
    cell_count = tile_rows * tile_cols
    cot_masked = (cotangent[0] * mask_bf[None]).reshape(channels, cell_count)
    out_flat, d_conv, grad_expand, grad_reduce, grad_gain = cell_pass(
        conv_out.reshape(channels, cell_count),
        state_tile.reshape(channels, cell_count),
        cot_masked,
        ocean_mask.astype(jnp.float32).reshape(cell_count),
        norm_gain,
        expand_weight,
        reduce_weight,
    )
    grad_depthwise = depthwise_grad(
        d_conv.reshape(channels, tile_rows, tile_cols), padded, tile_rows, tile_cols
    )
    grad_scale = 1.0 / math.sqrt(lax.axis_size("ens") * lat_count * lon_count * cell_count)
    grad_expand = grad_expand * grad_scale
    grad_reduce = grad_reduce * grad_scale
    grad_gain = grad_gain * grad_scale
    grad_depthwise = grad_depthwise * grad_scale
    width = grad_expand.shape[1]
    small = jnp.concatenate([grad_depthwise, grad_gain[None]], axis=0).reshape(-1)
    small_rows = -(-small.shape[0] // width)
    small_rows += -small_rows % 8
    small = jnp.pad(small, (0, small_rows * width - small.shape[0])).reshape(small_rows, width)
    packed = jnp.concatenate([grad_expand, grad_reduce.T, small], axis=0)
    packed = tree_psum(packed, REDUCE_ORDER, jnp.bfloat16)
    grad_expand = packed[:channels].astype(jnp.float32)
    grad_reduce = packed[channels : 2 * channels].T.astype(jnp.float32)
    small = packed[2 * channels :].reshape(-1)[: channels * (KS * KS + 1)].reshape(-1, channels)
    grad_depthwise = small[: KS * KS].T.astype(jnp.float32)
    grad_gain = small[KS * KS].astype(jnp.float32)
    next_state = out_flat.reshape(channels, tile_rows, tile_cols)[None]
    return (next_state, grad_depthwise, grad_gain, grad_expand, grad_reduce)


def solution(mesh):
    ens, lon, lat = (mesh.shape[name] for name in ("ens", "lon", "lat"))
    fine = Mesh(mesh.devices.reshape(ens, 2, lon // 4, 2, lat), ("ens",) + LON + ("lat",))
    return jax.shard_map(
        body,
        mesh=fine,
        in_specs=(
            P("ens", None, "lat", LON),
            P("lat", LON),
            P(),
            P(),
            P(),
            P(),
            P("ens", None, "lat", LON),
        ),
        out_specs=(P("ens", None, "lat", LON), P(), P(), P(), P()),
        check_vma=False,
    )
```

```python
import math

import jax
import jax.numpy as jnp
from jax import lax
from jax.sharding import Mesh, PartitionSpec as P

KS = 7


norm_eps = 1e-06
root_half = 0.7071067811865476
gauss_norm = 0.3989422804014327


def with_halo(cells, sides, width):
    for axis, dim in sides:
        count = lax.axis_size(axis)
        head = lax.slice_in_dim(cells, 0, width, axis=dim)
        tail = lax.slice_in_dim(cells, cells.shape[dim] - width, cells.shape[dim], axis=dim)
        cells = jnp.concatenate(
            [
                lax.ppermute(tail, axis, [(i, (i + 1) % count) for i in range(count)]),
                cells,
                lax.ppermute(head, axis, [((i + 1) % count, i) for i in range(count)]),
            ],
            axis=dim,
        )
    return cells


def swapped(array, axis, stride):
    return lax.ppermute(array, axis, [(i, i ^ 1 << stride) for i in range(lax.axis_size(axis))])


def mirrored_across(array, axis):
    count = lax.axis_size(axis)
    return lax.ppermute(array, axis, [(i, count - 1 - i) for i in range(count)])


LON = ("lon_z", "lon_y", "lon_c")
REDUCE_ORDER = (("lon_c", 0), ("lat", None), ("ens", None), ("lon_z", 0), ("lon_y", None))


def spread(array, axis):
    count = lax.axis_size(axis)
    copies = jnp.broadcast_to(array[None], (count,) + array.shape)
    return lax.all_to_all(copies, axis, 0, 0, tiled=False)


def tree_psum(flat, steps, gather_dtype):
    scattered = []
    for axis, bit in steps:
        rows = flat.shape[0]
        if bit is None:
            count = lax.axis_size(axis)
            if rows % count == 0:
                chunks = flat.reshape((count, rows // count) + flat.shape[1:])
                flat = lax.all_to_all(chunks, axis, 0, 0, tiled=False).sum(0)
                scattered.append((axis, bit))
            else:
                flat = spread(flat, axis).sum(0)
            continue
        if (1 << bit) >= lax.axis_size(axis):
            continue
        upper = (lax.axis_index(axis) >> bit) & 1
        if rows % 2 == 0 and rows >= 8:
            half = rows // 2
            keep = lax.dynamic_slice_in_dim(flat, upper * half, half, 0)
            send = lax.dynamic_slice_in_dim(flat, (1 - upper) * half, half, 0)
            flat = keep + swapped(send, axis, bit)
            scattered.append((axis, bit))
        else:
            flat = flat + swapped(flat, axis, bit)
    flat = flat.astype(gather_dtype)
    for axis, bit in reversed(scattered):
        if bit is None:
            gathered = spread(flat, axis)
            flat = gathered.reshape((-1,) + flat.shape[1:])
            continue
        upper = (lax.axis_index(axis) >> bit) & 1
        other = swapped(flat, axis, bit)
        rows = flat.shape[0]
        both = jnp.zeros((2 * rows,) + flat.shape[1:], flat.dtype)
        both = lax.dynamic_update_slice_in_dim(both, flat, upper * rows, 0)
        flat = lax.dynamic_update_slice_in_dim(both, other, (1 - upper) * rows, 0)
    return flat


def depthwise(padded, dw_weight, out_rows, out_cols):
    conv_sum = jnp.zeros((padded.shape[0], out_rows, out_cols), jnp.float32)
    for shift_a in range(KS):
        for shift_b in range(KS):
            tap_weight = dw_weight[:, shift_a * KS + shift_b][:, None, None]
            window = padded[:, shift_a : shift_a + out_rows, shift_b : shift_b + out_cols].astype(
                jnp.float32
            )
            conv_sum = conv_sum + tap_weight * window
    return conv_sum


def depthwise_grad(d_conv, padded, out_rows, out_cols):
    columns = []
    for shift_a in range(KS):
        for shift_b in range(KS):
            window = padded[:, shift_a : shift_a + out_rows, shift_b : shift_b + out_cols].astype(
                jnp.float32
            )
            columns.append(jnp.sum(d_conv * window, axis=(1, 2)))
    return jnp.stack(columns, axis=0)


def cell_pass(conv_blk, state_blk, cot_blk, mask_blk, norm_gain, expand_weight, reduce_weight):
    chan_mean = jnp.mean(conv_blk, axis=0, keepdims=True)
    centred = conv_blk - chan_mean
    chan_var = jnp.mean(centred * centred, axis=0, keepdims=True)
    inv_std = lax.rsqrt(chan_var + norm_eps)
    normed = centred * inv_std
    scaled = (normed * norm_gain[:, None]).astype(jnp.bfloat16)
    pre_act = jnp.dot(expand_weight.T, scaled, preferred_element_type=jnp.float32)
    normal_cdf = 0.5 * (1.0 + lax.erf(pre_act * root_half))
    normal_pdf = jnp.exp(-0.5 * pre_act * pre_act) * gauss_norm
    hidden = (pre_act * normal_cdf).astype(jnp.bfloat16)
    gelu_slope = normal_cdf + pre_act * normal_pdf
    branch = jnp.dot(reduce_weight.T, hidden, preferred_element_type=jnp.float32)
    out_blk = ((state_blk.astype(jnp.float32) + branch) * mask_blk[None, :]).astype(jnp.bfloat16)
    grad_reduce = jnp.dot(hidden, cot_blk.T, preferred_element_type=jnp.float32)
    d_hidden = jnp.dot(reduce_weight, cot_blk, preferred_element_type=jnp.float32)
    d_pre = (d_hidden * gelu_slope).astype(jnp.bfloat16)
    grad_expand = jnp.dot(scaled, d_pre.T, preferred_element_type=jnp.float32)
    d_scaled = jnp.dot(expand_weight, d_pre, preferred_element_type=jnp.float32)
    grad_gain = jnp.sum(d_scaled * normed, axis=1)
    d_normed = d_scaled * norm_gain[:, None]
    d_conv = inv_std * (
        d_normed
        - jnp.mean(d_normed, axis=0, keepdims=True)
        - normed * jnp.mean(d_normed * normed, axis=0, keepdims=True)
    )
    return (out_blk, d_conv, grad_expand, grad_reduce, grad_gain)


def body(ocean_state, ocean_mask, dw_weight, norm_gain, expand_weight, reduce_weight, cotangent):
    state_tile = ocean_state[0]
    channels = state_tile.shape[0]
    tile_rows = state_tile.shape[1]
    tile_cols = state_tile.shape[2]
    margin = KS // 2
    mask_bf = ocean_mask.astype(jnp.bfloat16)
    masked = state_tile * mask_bf[None]
    padded = with_halo(masked, ((LON, 2), ("lat", 1)), margin)
    lat_now = lax.axis_index("lat")
    lat_count = lax.axis_size("lat")
    lon_count = lax.axis_size(LON)
    top_strip = padded[:, tile_rows : tile_rows + margin, :][:, ::-1, ::-1]
    mirrored = mirrored_across(top_strip, LON)
    north_rows = jnp.where(lat_now == lat_count - 1, mirrored, padded[:, tile_rows + margin :, :])
    south_rows = jnp.where(lat_now == 0, jnp.zeros_like(top_strip), padded[:, :margin, :])
    padded = jnp.concatenate(
        [south_rows, padded[:, margin : tile_rows + margin, :], north_rows], axis=1
    )
    conv_out = depthwise(padded, dw_weight, tile_rows, tile_cols)
    cell_count = tile_rows * tile_cols
    cot_masked = (cotangent[0] * mask_bf[None]).reshape(channels, cell_count)
    out_flat, d_conv, grad_expand, grad_reduce, grad_gain = cell_pass(
        conv_out.reshape(channels, cell_count),
        state_tile.reshape(channels, cell_count),
        cot_masked,
        ocean_mask.astype(jnp.float32).reshape(cell_count),
        norm_gain,
        expand_weight,
        reduce_weight,
    )
    grad_depthwise = depthwise_grad(
        d_conv.reshape(channels, tile_rows, tile_cols), padded, tile_rows, tile_cols
    )
    grad_scale = 1.0 / math.sqrt(lax.axis_size("ens") * lat_count * lon_count * cell_count)
    grad_expand = grad_expand * grad_scale
    grad_reduce = grad_reduce * grad_scale
    grad_gain = grad_gain * grad_scale
    grad_depthwise = grad_depthwise * grad_scale
    width = grad_expand.shape[1]
    small = jnp.concatenate([grad_depthwise, grad_gain[None]], axis=0).reshape(-1)
    small_rows = -(-small.shape[0] // width)
    small_rows += -small_rows % 8
    small = jnp.pad(small, (0, small_rows * width - small.shape[0])).reshape(small_rows, width)
    packed = jnp.concatenate([grad_expand, grad_reduce.T, small], axis=0)
    packed = tree_psum(packed, REDUCE_ORDER, jnp.bfloat16)
    grad_expand = packed[:channels].astype(jnp.float32)
    grad_reduce = packed[channels : 2 * channels].T.astype(jnp.float32)
    small = packed[2 * channels :].reshape(-1)[: channels * (KS * KS + 1)].reshape(-1, channels)
    grad_depthwise = small[: KS * KS].T.astype(jnp.float32)
    grad_gain = small[KS * KS].astype(jnp.float32)
    next_state = out_flat.reshape(channels, tile_rows, tile_cols)[None]
    return (next_state, grad_depthwise, grad_gain, grad_expand, grad_reduce)


def solution(mesh):
    ens, lon, lat = (mesh.shape[name] for name in ("ens", "lon", "lat"))
    fine = Mesh(mesh.devices.reshape(ens, 2, lon // 4, 2, lat), ("ens",) + LON + ("lat",))
    return jax.shard_map(
        body,
        mesh=fine,
        in_specs=(
            P("ens", None, "lat", LON),
            P("lat", LON),
            P(),
            P(),
            P(),
            P(),
            P("ens", None, "lat", LON),
        ),
        out_specs=(P("ens", None, "lat", LON), P(), P(), P(), P()),
        check_vma=False,
    )
```

```python
import math

import jax
import jax.numpy as jnp
from jax import lax
from jax.sharding import Mesh, PartitionSpec as P

KS = 7


norm_eps = 1e-06
root_half = 0.7071067811865476
gauss_norm = 0.3989422804014327


def with_halo(cells, sides, width):
    for axis, dim in sides:
        count = lax.axis_size(axis)
        head = lax.slice_in_dim(cells, 0, width, axis=dim)
        tail = lax.slice_in_dim(cells, cells.shape[dim] - width, cells.shape[dim], axis=dim)
        cells = jnp.concatenate(
            [
                lax.ppermute(tail, axis, [(i, (i + 1) % count) for i in range(count)]),
                cells,
                lax.ppermute(head, axis, [((i + 1) % count, i) for i in range(count)]),
            ],
            axis=dim,
        )
    return cells


def swapped(array, axis, stride):
    return lax.ppermute(array, axis, [(i, i ^ 1 << stride) for i in range(lax.axis_size(axis))])


def mirrored_across(array, axis):
    count = lax.axis_size(axis)
    return lax.ppermute(array, axis, [(i, count - 1 - i) for i in range(count)])


LON = ("lon_z", "lon_y", "lon_c")
REDUCE_ORDER = (("lon_c", 0), ("lat", None), ("ens", None), ("lon_z", 0), ("lon_y", None))


def spread(array, axis):
    count = lax.axis_size(axis)
    copies = jnp.broadcast_to(array[None], (count,) + array.shape)
    return lax.all_to_all(copies, axis, 0, 0, tiled=False)


def tree_psum(flat, steps, gather_dtype):
    scattered = []
    for axis, bit in steps:
        rows = flat.shape[0]
        if bit is None:
            count = lax.axis_size(axis)
            if rows % count == 0:
                chunks = flat.reshape((count, rows // count) + flat.shape[1:])
                flat = lax.all_to_all(chunks, axis, 0, 0, tiled=False).sum(0)
                scattered.append((axis, bit))
            else:
                flat = spread(flat, axis).sum(0)
            continue
        if (1 << bit) >= lax.axis_size(axis):
            continue
        upper = (lax.axis_index(axis) >> bit) & 1
        if rows % 2 == 0 and rows >= 8:
            half = rows // 2
            keep = lax.dynamic_slice_in_dim(flat, upper * half, half, 0)
            send = lax.dynamic_slice_in_dim(flat, (1 - upper) * half, half, 0)
            flat = keep + swapped(send, axis, bit)
            scattered.append((axis, bit))
        else:
            flat = flat + swapped(flat, axis, bit)
    flat = flat.astype(gather_dtype)
    for axis, bit in reversed(scattered):
        if bit is None:
            gathered = spread(flat, axis)
            flat = gathered.reshape((-1,) + flat.shape[1:])
            continue
        upper = (lax.axis_index(axis) >> bit) & 1
        other = swapped(flat, axis, bit)
        first = jnp.where(upper == 0, flat, other)
        second = jnp.where(upper == 0, other, flat)
        flat = jnp.concatenate([first, second])
    return flat


def depthwise(padded, dw_weight, out_rows, out_cols):
    conv_sum = jnp.zeros((padded.shape[0], out_rows, out_cols), jnp.float32)
    for shift_a in range(KS):
        for shift_b in range(KS):
            tap_weight = dw_weight[:, shift_a * KS + shift_b][:, None, None]
            window = padded[:, shift_a : shift_a + out_rows, shift_b : shift_b + out_cols].astype(
                jnp.float32
            )
            conv_sum = conv_sum + tap_weight * window
    return conv_sum


def depthwise_grad(d_conv, padded, out_rows, out_cols):
    columns = []
    for shift_a in range(KS):
        for shift_b in range(KS):
            window = padded[:, shift_a : shift_a + out_rows, shift_b : shift_b + out_cols].astype(
                jnp.float32
            )
            columns.append(jnp.sum(d_conv * window, axis=(1, 2)))
    return jnp.stack(columns, axis=0)


def cell_pass(conv_blk, state_blk, cot_blk, mask_blk, norm_gain, expand_weight, reduce_weight):
    chan_mean = jnp.mean(conv_blk, axis=0, keepdims=True)
    centred = conv_blk - chan_mean
    chan_var = jnp.mean(centred * centred, axis=0, keepdims=True)
    inv_std = lax.rsqrt(chan_var + norm_eps)
    normed = centred * inv_std
    scaled = (normed * norm_gain[:, None]).astype(jnp.bfloat16)
    pre_act = jnp.dot(expand_weight.T, scaled, preferred_element_type=jnp.float32)
    normal_cdf = 0.5 * (1.0 + lax.erf(pre_act * root_half))
    normal_pdf = jnp.exp(-0.5 * pre_act * pre_act) * gauss_norm
    hidden = (pre_act * normal_cdf).astype(jnp.bfloat16)
    gelu_slope = normal_cdf + pre_act * normal_pdf
    branch = jnp.dot(reduce_weight.T, hidden, preferred_element_type=jnp.float32)
    out_blk = ((state_blk.astype(jnp.float32) + branch) * mask_blk[None, :]).astype(jnp.bfloat16)
    grad_reduce = jnp.dot(hidden, cot_blk.T, preferred_element_type=jnp.float32)
    d_hidden = jnp.dot(reduce_weight, cot_blk, preferred_element_type=jnp.float32)
    d_pre = (d_hidden * gelu_slope).astype(jnp.bfloat16)
    grad_expand = jnp.dot(scaled, d_pre.T, preferred_element_type=jnp.float32)
    d_scaled = jnp.dot(expand_weight, d_pre, preferred_element_type=jnp.float32)
    grad_gain = jnp.sum(d_scaled * normed, axis=1)
    d_normed = d_scaled * norm_gain[:, None]
    d_conv = inv_std * (
        d_normed
        - jnp.mean(d_normed, axis=0, keepdims=True)
        - normed * jnp.mean(d_normed * normed, axis=0, keepdims=True)
    )
    return (out_blk, d_conv, grad_expand, grad_reduce, grad_gain)


def body(ocean_state, ocean_mask, dw_weight, norm_gain, expand_weight, reduce_weight, cotangent):
    state_tile = ocean_state[0]
    channels = state_tile.shape[0]
    tile_rows = state_tile.shape[1]
    tile_cols = state_tile.shape[2]
    margin = KS // 2
    mask_bf = ocean_mask.astype(jnp.bfloat16)
    masked = state_tile * mask_bf[None]
    padded = with_halo(masked, ((LON, 2), ("lat", 1)), margin)
    lat_now = lax.axis_index("lat")
    lat_count = lax.axis_size("lat")
    lon_count = lax.axis_size(LON)
    top_strip = padded[:, tile_rows : tile_rows + margin, :][:, ::-1, ::-1]
    mirrored = mirrored_across(top_strip, LON)
    north_rows = jnp.where(lat_now == lat_count - 1, mirrored, padded[:, tile_rows + margin :, :])
    south_rows = jnp.where(lat_now == 0, jnp.zeros_like(top_strip), padded[:, :margin, :])
    padded = jnp.concatenate(
        [south_rows, padded[:, margin : tile_rows + margin, :], north_rows], axis=1
    )
    conv_out = depthwise(padded, dw_weight, tile_rows, tile_cols)
    cell_count = tile_rows * tile_cols
    cot_masked = (cotangent[0] * mask_bf[None]).reshape(channels, cell_count)
    out_flat, d_conv, grad_expand, grad_reduce, grad_gain = cell_pass(
        conv_out.reshape(channels, cell_count),
        state_tile.reshape(channels, cell_count),
        cot_masked,
        ocean_mask.astype(jnp.float32).reshape(cell_count),
        norm_gain,
        expand_weight,
        reduce_weight,
    )
    grad_depthwise = depthwise_grad(
        d_conv.reshape(channels, tile_rows, tile_cols), padded, tile_rows, tile_cols
    )
    grad_scale = 1.0 / math.sqrt(lax.axis_size("ens") * lat_count * lon_count * cell_count)
    grad_expand = grad_expand * grad_scale
    grad_reduce = grad_reduce * grad_scale
    grad_gain = grad_gain * grad_scale
    grad_depthwise = grad_depthwise * grad_scale
    width = grad_expand.shape[1]
    small = jnp.concatenate([grad_depthwise, grad_gain[None]], axis=0).reshape(-1)
    small_rows = -(-small.shape[0] // width)
    small_rows += -small_rows % 8
    small = jnp.pad(small, (0, small_rows * width - small.shape[0])).reshape(small_rows, width)
    packed = jnp.concatenate([grad_expand, grad_reduce.T, small], axis=0)
    packed = tree_psum(packed, REDUCE_ORDER, jnp.bfloat16)
    grad_expand = packed[:channels].astype(jnp.float32)
    grad_reduce = packed[channels : 2 * channels].T.astype(jnp.float32)
    small = packed[2 * channels :].reshape(-1)[: channels * (KS * KS + 1)].reshape(-1, channels)
    grad_depthwise = small[: KS * KS].T.astype(jnp.float32)
    grad_gain = small[KS * KS].astype(jnp.float32)
    next_state = out_flat.reshape(channels, tile_rows, tile_cols)[None]
    return (next_state, grad_depthwise, grad_gain, grad_expand, grad_reduce)


def solution(mesh):
    ens, lon, lat = (mesh.shape[name] for name in ("ens", "lon", "lat"))
    fine = Mesh(mesh.devices.reshape(ens, 2, lon // 4, 2, lat), ("ens",) + LON + ("lat",))
    return jax.shard_map(
        body,
        mesh=fine,
        in_specs=(
            P("ens", None, "lat", LON),
            P("lat", LON),
            P(),
            P(),
            P(),
            P(),
            P("ens", None, "lat", LON),
        ),
        out_specs=(P("ens", None, "lat", LON), P(), P(), P(), P()),
        check_vma=False,
    )
```
